32 devices in a mesh: enc: 4 (over y, x), pool: 8 (over z, core).
Axes of the slice: x: 2, y: 2, z: 4, core: 2. Of those that a mesh axis runs over, the one named last changes fastest.
Arguments:
- encoded: bfloat16 [2048, 32, 128], P('pool', 'enc'), may hold values from -6 to 6
- slot_items: int32 [2048], replicated, may hold values from 0 to 2047, as said below
- lengths: int32 [2048], P(('enc', 'pool')), may hold values from 1 to 32
- token_mask: int32 [2048, 32], P(('enc', 'pool')), may hold values 0 or 1
Outputs:
- scores: float32 [2048, 192], P(('enc', 'pool'))
The draws below stay inside these ranges and needn't reach their ends.
Inputs may be any that keep to these rules, and one draw needn't show every extreme that they name: `slot_items`: each item appears in exactly one slot. The slots d * 64 + p * 8 + j, for j below 8, hold items p * 256 to (p + 1) * 256 - 1, those whose encoder rows lie on pool index p.
All inputs are finite; a program needn't handle non-finite values. No bound on the sum of `token_mask` on one device may be relied on, other than what follows from the above.
Results may differ from the reference program's by a relative error of at most 0.00057.
Values may be sent and summed in bfloat16 or wider, within the bound.
No kernel may reach another device: no remote copies, remote signals or barrier semaphores. Data moves between devices by JAX's collectives and lax.ppermute only.
A program may use at most 64 MiB of HBM per device.

```python
import jax
import jax.numpy as jnp
from jax import lax

H = 128
TOK = 32
ITEM_DEV = 64
ITEMS = 2048
PER = 8
GROUP = 256
N_ENC = 4
N_POOL = 8


def draw_slot_items(key, part):
    groups = ITEMS // GROUP
    owners = ITEMS // ITEM_DEV
    keys = jax.random.split(key, groups)
    orders = jax.vmap(lambda single: jax.random.permutation(single, GROUP))(keys).astype(jnp.int32)
    offsets = jnp.arange(groups, dtype=jnp.int32)[:, None] * GROUP
    placed = (orders + offsets).reshape(groups, owners, PER)
    return jnp.transpose(placed, (1, 0, 2)).reshape(ITEMS).astype(jnp.int32)


def plant(values, own_key, smallest, largest):
    longest = values.shape.index(max(values.shape))
    spots = []
    for shift in (0, 1):
        where = [jax.random.randint(jax.random.fold_in(own_key, axis), (), 0, length) for axis, length in enumerate(values.shape)]
        where[longest] = (where[longest] + shift) % values.shape[longest]
        spots.append(tuple(where))
    return values.at[spots[0]].set(smallest).at[spots[1]].set(largest)


def block_levels(key, shape, shards, smallest, largest):
    def one(dim, blocks):
        draws = jax.random.uniform(jax.random.fold_in(jax.random.fold_in(key, 6), dim), (blocks,), jnp.float32, smallest / len(shards), largest / len(shards))
        return jnp.repeat(jnp.exp(draws), shape[dim] // blocks).reshape((-1,) + (1,) * (len(shape) - dim - 1))

    factor_of = one(*shards[0])
    for cut in shards[1:]:
        factor_of = factor_of * one(*cut)
    return factor_of


def gaussian(key, dims, scale, most, cuts=(), kind=jnp.bfloat16):
    gain = block_levels(key, dims, cuts, -0.22, 0.18) if cuts else 1.0
    array = jax.random.normal(key, dims, jnp.float32) * scale * gain
    return jnp.minimum(jnp.maximum(array, -most), most).astype(kind)


def setup_inputs(seed: int = 0) -> dict:
    streams_of = jax.random.split(jax.random.key(seed), 5)
    return {
        "encoded": gaussian(streams_of[0], (ITEMS, TOK, H), 1.0, 6.0, ((0, 8), (1, 4))),
        "slot_items": draw_slot_items(jax.random.fold_in(streams_of[4], 71), 0),
        "lengths": plant(jax.random.randint(streams_of[2], (ITEMS,), 1, TOK + 1), jax.random.fold_in(streams_of[2], 1), 1, TOK).astype(jnp.int32),
        "token_mask": plant((jax.random.randint(streams_of[3], (ITEMS, TOK), 0, 4) < 3).astype(jnp.int32), jax.random.fold_in(streams_of[3], 1), 0, 1),
    }


def chamfer(query, query_valid, other, other_valid):
    dots = jnp.dot(query, other.T, preferred_element_type=jnp.float32)
    dots = dots.reshape(ITEM_DEV, TOK, ITEM_DEV, TOK)
    fore = lax.optimization_barrier(jnp.max(jnp.where(other_valid[None, None] > 0, dots, -4.0), axis=3))
    fore = lax.optimization_barrier(jnp.sum(jnp.where(query_valid[:, :, None] > 0, fore, 0.0), axis=1))
    back = lax.optimization_barrier(jnp.max(jnp.where(query_valid[:, :, None, None] > 0, dots, -4.0), axis=1))
    back = lax.optimization_barrier(jnp.sum(jnp.where(other_valid[None] > 0, back, 0.0), axis=2))
    return 0.5 * (fore + back)

def reference(encoded, slot_items, lengths, token_mask):
    slotted = encoded[slot_items]
    values = slotted.astype(jnp.float32)
    normed = (values / jnp.sqrt(lax.optimization_barrier(jnp.sum(values * values, axis=-1, keepdims=True)) + 1e-06)).astype(jnp.bfloat16)
    position = jnp.arange(TOK, dtype=jnp.int32)[None, :]
    valid = ((position < lengths[:, None]) & ((position == 0) | (token_mask == 1))).astype(jnp.int32)
    owners = N_ENC * N_POOL
    blocks = normed.reshape(owners, ITEM_DEV * TOK, H)
    valid_blocks = valid.reshape(owners, ITEM_DEV, TOK)

    def one_owner(owner):
        tiles = []
        for bit in range(3):
            mate = jnp.bitwise_xor(owner, jnp.int32(1 << bit))
            tiles.append(chamfer(blocks[owner], valid_blocks[owner], blocks[mate], valid_blocks[mate]))
        return jnp.concatenate(tiles, axis=1)
    scores = lax.map(one_owner, jnp.arange(owners, dtype=jnp.int32))
    return scores.reshape(ITEMS, 3 * ITEM_DEV)
```

```python
import jax
import jax.numpy as jnp
from jax import lax
from jax.sharding import PartitionSpec as P


def from_partner(array, axis, stride):
    return lax.ppermute(array, axis, [(i, i ^ 1 << stride) for i in range(lax.axis_size(axis))])


def tile_scores(block, bias, other, other_bias, tok):
    query_items = block.shape[0] // tok
    other_items = other.shape[0] // tok
    width = block.shape[1]
    rows = min(32, query_items)
    blocks = query_items // rows
    other_tr = jnp.transpose(other.reshape(other_items, tok, width), (1, 0, 2))
    other_float = other_bias.astype(jnp.float32)
    other_add_tr = jnp.transpose(other_float.reshape(other_items, tok), (1, 0))[:, :, None]
    other_owner = (jnp.arange(other_items * tok, dtype=jnp.int32) // tok)[:, None] == jnp.arange(
        other_items, dtype=jnp.int32
    )[None, :]
    other_select = jnp.where((other_bias == 0)[:, None] & other_owner, 1.0, 0.0).astype(jnp.float32)
    query_flat = block.reshape(blocks, rows * tok, width)
    query_tr = jnp.transpose(block.reshape(blocks, rows, tok, width), (0, 2, 1, 3))
    bias_float = bias.astype(jnp.float32).reshape(blocks, rows, tok)
    query_add_tr = jnp.transpose(bias_float, (0, 2, 1))[..., None]
    query_valid = (bias == 0).reshape(blocks, rows * tok)
    query_owner = (jnp.arange(rows * tok, dtype=jnp.int32) // tok)[:, None] == jnp.arange(
        rows, dtype=jnp.int32
    )[None, :]

    def one_block(operands):
        flat, turned, adding, kept = operands
        dots_fore = jnp.einsum("ubh,qh->ubq", other_tr, flat, preferred_element_type=jnp.float32)
        fore = jnp.max(dots_fore + other_add_tr, axis=0)
        select = jnp.where(kept[:, None] & query_owner, 1.0, 0.0).astype(jnp.float32)
        fore = jnp.dot(
            fore, select, precision=lax.Precision.HIGHEST, preferred_element_type=jnp.float32
        )
        dots_back = jnp.einsum("trh,ch->trc", turned, other, preferred_element_type=jnp.float32)
        back = jnp.max(dots_back + adding, axis=0)
        back = jnp.dot(
            back, other_select, precision=lax.Precision.HIGHEST, preferred_element_type=jnp.float32
        )
        return 0.5 * (fore.T + back)

    result = lax.map(one_block, (query_flat, query_tr, query_add_tr, query_valid))
    return result.reshape(query_items, other_items)


def shards(encoded, slot_items, lengths, token_mask):
    n_enc = lax.axis_size("enc")
    n_pool = lax.axis_size("pool")
    owners = n_enc * n_pool
    group = encoded.shape[0]
    toks = encoded.shape[1]
    width = encoded.shape[2]
    items_dev = lengths.shape[0]
    per = items_dev // n_pool
    pool_index = lax.axis_index("pool")
    table = slot_items.reshape(owners, n_pool, per)
    mine = lax.dynamic_index_in_dim(table, pool_index, 1, keepdims=False) - pool_index * group
    outgoing = jnp.take(encoded, mine, axis=0)
    arrived = lax.all_to_all(outgoing, ("enc", "pool"), split_axis=0, concat_axis=0, tiled=True)
    arrived = arrived.reshape(n_enc, n_pool, per, toks, width)
    tok = n_enc * toks
    slotted = jnp.transpose(arrived, (1, 2, 0, 3, 4)).reshape(items_dev, tok, width)
    values = slotted.astype(jnp.float32)
    normed = (values / jnp.sqrt(jnp.sum(values * values, axis=-1, keepdims=True) + 1e-06)).astype(
        jnp.bfloat16
    )
    position = jnp.arange(tok, dtype=jnp.int32)[None, :]
    valid = (position < lengths[:, None]) & ((position == 0) | (token_mask == 1))
    bias = jnp.where(valid, 0.0, -4.0).astype(jnp.bfloat16).reshape(-1)
    block = normed.reshape(items_dev * tok, width)
    n_tok = items_dev * tok
    packed = jnp.concatenate([block, bias.reshape(-1, width)], axis=0)

    pool_index = lax.axis_index("pool")
    parity = (pool_index ^ (pool_index >> 1) ^ (pool_index >> 2)) & 1
    is_a = (pool_index & 1) == 0

    def par(p):
        return (p ^ (p >> 1) ^ (p >> 2)) & 1

    send_pairs = [(p, p ^ (4 if par(p) else 2)) for p in range(n_pool)]
    back_pairs = [(t, s) for s, t in send_pairs]
    chip_pairs = [(p, p ^ 1) for p in range(n_pool)]

    z_recv = lax.ppermute(packed, "pool", send_pairs)
    c_recv = lax.ppermute(packed, "pool", chip_pairs)

    half = n_tok // 2
    c_blk, c_bias = c_recv[:n_tok], c_recv[n_tok:].reshape(-1)
    query = jnp.where(is_a, block[:half], c_blk[half:])
    query_bias = jnp.where(is_a, bias[:half], c_bias[half:])
    other = jnp.where(is_a, c_blk, block)
    other_bias = jnp.where(is_a, c_bias, bias)
    part = tile_scores(query, query_bias, other, other_bias, tok)
    part_recv = lax.ppermute(part, "pool", chip_pairs)
    joined = jnp.where(
        is_a,
        jnp.concatenate([part, part_recv], axis=0),
        jnp.concatenate([part_recv, part], axis=0),
    )
    tile0 = jnp.where(is_a, joined, joined.T)

    z_blk, z_bias = z_recv[:n_tok], z_recv[n_tok:].reshape(-1)
    tile_z = tile_scores(block, bias, z_blk, z_bias, tok)
    tile_back = lax.ppermute(tile_z.T, "pool", back_pairs)
    via_bit1 = parity == 1
    col1 = jnp.where(via_bit1, tile_z, tile_back)
    col2 = jnp.where(via_bit1, tile_back, tile_z)
    return jnp.concatenate([tile0, col1, col2], axis=1)


def solution(mesh):
    in_specs = (P("pool", "enc", None), P(), P(("enc", "pool")), P(("enc", "pool"), None))
    out_specs = P(("enc", "pool"), None)
    return jax.shard_map(shards, mesh=mesh, in_specs=in_specs, out_specs=out_specs, check_vma=False)
```

```python
import jax
import jax.numpy as jnp
from jax import lax
from jax.sharding import PartitionSpec as P


def from_partner(array, axis, stride):
    return lax.ppermute(array, axis, [(i, i ^ 1 << stride) for i in range(lax.axis_size(axis))])


def tile_scores(block, bias, other, other_bias, tok):
    query_items = block.shape[0] // tok
    other_items = other.shape[0] // tok
    width = block.shape[1]
    rows = min(32, query_items)
    blocks = query_items // rows
    other_tr = jnp.transpose(other.reshape(other_items, tok, width), (1, 0, 2))
    other_float = other_bias.astype(jnp.float32)
    other_add_tr = jnp.transpose(other_float.reshape(other_items, tok), (1, 0))[:, :, None]
    other_owner = (jnp.arange(other_items * tok, dtype=jnp.int32) // tok)[:, None] == jnp.arange(
        other_items, dtype=jnp.int32
    )[None, :]
    other_select = jnp.where((other_bias == 0)[:, None] & other_owner, 1.0, 0.0).astype(jnp.float32)
    query_flat = block.reshape(blocks, rows * tok, width)
    query_tr = jnp.transpose(block.reshape(blocks, rows, tok, width), (0, 2, 1, 3))
    bias_float = bias.astype(jnp.float32).reshape(blocks, rows, tok)
    query_add_tr = jnp.transpose(bias_float, (0, 2, 1))[..., None]
    query_valid = (bias == 0).reshape(blocks, rows * tok)
    query_owner = (jnp.arange(rows * tok, dtype=jnp.int32) // tok)[:, None] == jnp.arange(
        rows, dtype=jnp.int32
    )[None, :]

    def one_block(operands):
        flat, turned, adding, kept = operands
        dots_fore = jnp.einsum("ubh,qh->ubq", other_tr, flat, preferred_element_type=jnp.float32)
        fore = jnp.max(dots_fore + other_add_tr, axis=0)
        select = jnp.where(kept[:, None] & query_owner, 1.0, 0.0).astype(jnp.float32)
        fore = jnp.dot(
            fore, select, precision=lax.Precision.HIGHEST, preferred_element_type=jnp.float32
        )
        dots_back = jnp.einsum("trh,ch->trc", turned, other, preferred_element_type=jnp.float32)
        back = jnp.max(dots_back + adding, axis=0)
        back = jnp.dot(
            back, other_select, precision=lax.Precision.HIGHEST, preferred_element_type=jnp.float32
        )
        return 0.5 * (fore.T + back)

    result = lax.map(one_block, (query_flat, query_tr, query_add_tr, query_valid))
    return result.reshape(query_items, other_items)


def shards(encoded, slot_items, lengths, token_mask):
    n_enc = lax.axis_size("enc")
    n_pool = lax.axis_size("pool")
    owners = n_enc * n_pool
    group = encoded.shape[0]
    toks = encoded.shape[1]
    width = encoded.shape[2]
    items_dev = lengths.shape[0]
    per = items_dev // n_pool
    pool_index = lax.axis_index("pool")
    enc_index = lax.axis_index("enc")
    table = slot_items.reshape(n_enc, n_pool, n_pool, per)
    mine = lax.dynamic_index_in_dim(table, pool_index, 2, keepdims=False) - pool_index * group
    order = jnp.transpose(mine, (1, 2, 0))
    outgoing = jnp.take(encoded, order, axis=0)
    across = lax.all_to_all(outgoing, "enc", split_axis=2, concat_axis=2, tiled=True)
    tok = n_enc * toks
    across = across.reshape(n_pool, per, tok, width)
    slotted = lax.all_to_all(across, "pool", split_axis=0, concat_axis=0, tiled=True)
    slotted = slotted.reshape(items_dev, tok, width)
    values = slotted.astype(jnp.float32)
    normed = (values / jnp.sqrt(jnp.sum(values * values, axis=-1, keepdims=True) + 1e-06)).astype(
        jnp.bfloat16
    )
    position = jnp.arange(tok, dtype=jnp.int32)[None, :]
    valid = (position < lengths[:, None]) & ((position == 0) | (token_mask == 1))
    bias = jnp.where(valid, 0.0, -4.0).astype(jnp.bfloat16).reshape(-1)
    block = normed.reshape(items_dev * tok, width)
    n_tok = items_dev * tok
    packed = jnp.concatenate([block, bias.reshape(-1, width)], axis=0)

    pool_index = lax.axis_index("pool")
    parity = (pool_index ^ (pool_index >> 1) ^ (pool_index >> 2)) & 1
    is_a = (pool_index & 1) == 0

    def par(p):
        return (p ^ (p >> 1) ^ (p >> 2)) & 1

    send_pairs = [(p, p ^ (4 if par(p) else 2)) for p in range(n_pool)]
    back_pairs = [(t, s) for s, t in send_pairs]
    chip_pairs = [(p, p ^ 1) for p in range(n_pool)]

    z_recv = lax.ppermute(packed, "pool", send_pairs)
    c_recv = lax.ppermute(packed, "pool", chip_pairs)

    half = n_tok // 2
    c_blk, c_bias = c_recv[:n_tok], c_recv[n_tok:].reshape(-1)
    query = jnp.where(is_a, block[:half], c_blk[half:])
    query_bias = jnp.where(is_a, bias[:half], c_bias[half:])
    other = jnp.where(is_a, c_blk, block)
    other_bias = jnp.where(is_a, c_bias, bias)
    part = tile_scores(query, query_bias, other, other_bias, tok)
    part_recv = lax.ppermute(part, "pool", chip_pairs)
    joined = jnp.where(
        is_a,
        jnp.concatenate([part, part_recv], axis=0),
        jnp.concatenate([part_recv, part], axis=0),
    )
    tile0 = jnp.where(is_a, joined, joined.T)

    z_blk, z_bias = z_recv[:n_tok], z_recv[n_tok:].reshape(-1)
    tile_z = tile_scores(block, bias, z_blk, z_bias, tok)
    tile_back = lax.ppermute(tile_z.T, "pool", back_pairs)
    via_bit1 = parity == 1
    col1 = jnp.where(via_bit1, tile_z, tile_back)
    col2 = jnp.where(via_bit1, tile_back, tile_z)
    return jnp.concatenate([tile0, col1, col2], axis=1)


def solution(mesh):
    in_specs = (P("pool", "enc", None), P(), P(("enc", "pool")), P(("enc", "pool"), None))
    out_specs = P(("enc", "pool"), None)
    return jax.shard_map(shards, mesh=mesh, in_specs=in_specs, out_specs=out_specs, check_vma=False)
```

```python
import jax
import jax.numpy as jnp
from jax import lax
from jax.sharding import PartitionSpec as P


def from_partner(array, axis, stride):
    return lax.ppermute(array, axis, [(i, i ^ 1 << stride) for i in range(lax.axis_size(axis))])


def tile_scores(block, bias, other, other_bias, tok):
    query_items = block.shape[0] // tok
    other_items = other.shape[0] // tok
    width = block.shape[1]
    rows = min(32, query_items)
    blocks = query_items // rows
    other_tr = jnp.transpose(other.reshape(other_items, tok, width), (1, 0, 2))
    other_float = other_bias.astype(jnp.float32)
    other_add_tr = jnp.transpose(other_float.reshape(other_items, tok), (1, 0))[:, :, None]
    other_valid = (other_bias == 0).reshape(other_items, tok)
    query_flat = block.reshape(blocks, rows * tok, width)
    query_tr = jnp.transpose(block.reshape(blocks, rows, tok, width), (0, 2, 1, 3))
    bias_float = bias.astype(jnp.float32).reshape(blocks, rows, tok)
    query_add_tr = jnp.transpose(bias_float, (0, 2, 1))[..., None]
    query_valid = (bias == 0).reshape(blocks, rows, tok)

    def one_block(operands):
        flat, turned, adding, kept = operands
        dots_fore = jnp.einsum("ubh,qh->ubq", other_tr, flat, preferred_element_type=jnp.float32)
        fore = jnp.max(dots_fore + other_add_tr, axis=0).reshape(other_items, rows, tok)
        fore = jnp.sum(jnp.where(kept[None], fore, 0.0), axis=2)
        dots_back = jnp.einsum("trh,ch->trc", turned, other, preferred_element_type=jnp.float32)
        back = jnp.max(dots_back + adding, axis=0).reshape(rows, other_items, tok)
        back = jnp.sum(jnp.where(other_valid[None], back, 0.0), axis=2)
        return 0.5 * (fore.T + back)

    result = lax.map(one_block, (query_flat, query_tr, query_add_tr, query_valid))
    return result.reshape(query_items, other_items)


def shards(encoded, slot_items, lengths, token_mask):
    n_enc = lax.axis_size("enc")
    n_pool = lax.axis_size("pool")
    owners = n_enc * n_pool
    group = encoded.shape[0]
    toks = encoded.shape[1]
    width = encoded.shape[2]
    items_dev = lengths.shape[0]
    per = items_dev // n_pool
    pool_index = lax.axis_index("pool")
    table = slot_items.reshape(owners, n_pool, per)
    mine = lax.dynamic_index_in_dim(table, pool_index, 1, keepdims=False) - pool_index * group
    outgoing = jnp.take(encoded, mine, axis=0)
    arrived = lax.all_to_all(outgoing, ("enc", "pool"), split_axis=0, concat_axis=0, tiled=True)
    arrived = arrived.reshape(n_enc, n_pool, per, toks, width)
    tok = n_enc * toks
    slotted = jnp.transpose(arrived, (1, 2, 0, 3, 4)).reshape(items_dev, tok, width)
    values = slotted.astype(jnp.float32)
    normed = (values / jnp.sqrt(jnp.sum(values * values, axis=-1, keepdims=True) + 1e-06)).astype(
        jnp.bfloat16
    )
    position = jnp.arange(tok, dtype=jnp.int32)[None, :]
    valid = (position < lengths[:, None]) & ((position == 0) | (token_mask == 1))
    bias = jnp.where(valid, 0.0, -4.0).astype(jnp.bfloat16).reshape(-1)
    block = normed.reshape(items_dev * tok, width)
    n_tok = items_dev * tok
    packed = jnp.concatenate([block, bias.reshape(-1, width)], axis=0)

    pool_index = lax.axis_index("pool")
    parity = (pool_index ^ (pool_index >> 1) ^ (pool_index >> 2)) & 1
    is_a = (pool_index & 1) == 0

    def par(p):
        return (p ^ (p >> 1) ^ (p >> 2)) & 1

    send_pairs = [(p, p ^ (4 if par(p) else 2)) for p in range(n_pool)]
    back_pairs = [(t, s) for s, t in send_pairs]
    chip_pairs = [(p, p ^ 1) for p in range(n_pool)]

    z_recv = lax.ppermute(packed, "pool", send_pairs)
    c_recv = lax.ppermute(packed, "pool", chip_pairs)

    half = n_tok // 2
    c_blk, c_bias = c_recv[:n_tok], c_recv[n_tok:].reshape(-1)
    query = jnp.where(is_a, block[:half], c_blk[half:])
    query_bias = jnp.where(is_a, bias[:half], c_bias[half:])
    other = jnp.where(is_a, c_blk, block)
    other_bias = jnp.where(is_a, c_bias, bias)
    part = tile_scores(query, query_bias, other, other_bias, tok)
    part_recv = lax.ppermute(part, "pool", chip_pairs)
    joined = jnp.where(
        is_a,
        jnp.concatenate([part, part_recv], axis=0),
        jnp.concatenate([part_recv, part], axis=0),
    )
    tile0 = jnp.where(is_a, joined, joined.T)

    z_blk, z_bias = z_recv[:n_tok], z_recv[n_tok:].reshape(-1)
    tile_z = tile_scores(block, bias, z_blk, z_bias, tok)
    tile_back = lax.ppermute(tile_z.T, "pool", back_pairs)
    via_bit1 = parity == 1
    col1 = jnp.where(via_bit1, tile_z, tile_back)
    col2 = jnp.where(via_bit1, tile_back, tile_z)
    return jnp.concatenate([tile0, col1, col2], axis=1)


def solution(mesh):
    in_specs = (P("pool", "enc", None), P(), P(("enc", "pool")), P(("enc", "pool"), None))
    out_specs = P(("enc", "pool"), None)
    return jax.shard_map(shards, mesh=mesh, in_specs=in_specs, out_specs=out_specs, check_vma=False)
```

```python
import jax
import jax.numpy as jnp
from jax import lax
from jax.sharding import PartitionSpec as P


def from_partner(array, axis, stride):
    return lax.ppermute(array, axis, [(i, i ^ 1 << stride) for i in range(lax.axis_size(axis))])


def tile_scores(block, bias, other, other_bias, tok):
    query_items = block.shape[0] // tok
    other_items = other.shape[0] // tok
    width = block.shape[1]
    rows = min(32, query_items)
    blocks = query_items // rows
    other_tr = jnp.transpose(other.reshape(other_items, tok, width), (1, 0, 2))
    other_float = other_bias.astype(jnp.float32)
    other_add_tr = jnp.transpose(other_float.reshape(other_items, tok), (1, 0))[:, :, None]
    other_valid = (other_bias == 0).reshape(other_items, tok)
    query_flat = block.reshape(blocks, rows * tok, width)
    query_tr = jnp.transpose(block.reshape(blocks, rows, tok, width), (0, 2, 1, 3))
    bias_float = bias.astype(jnp.float32).reshape(blocks, rows, tok)
    query_add_tr = jnp.transpose(bias_float, (0, 2, 1))[..., None]
    query_valid = (bias == 0).reshape(blocks, rows, tok)

    def one_block(operands):
        flat, turned, adding, kept = operands
        dots_fore = jnp.einsum("ubh,qh->ubq", other_tr, flat, preferred_element_type=jnp.float32)
        fore = jnp.max(dots_fore + other_add_tr, axis=0).reshape(other_items, rows, tok)
        fore = jnp.sum(jnp.where(kept[None], fore, 0.0), axis=2)
        dots_back = jnp.einsum("trh,ch->trc", turned, other, preferred_element_type=jnp.float32)
        back = jnp.max(dots_back + adding, axis=0).reshape(rows, other_items, tok)
        back = jnp.sum(jnp.where(other_valid[None], back, 0.0), axis=2)
        return 0.5 * (fore.T + back)

    result = lax.map(one_block, (query_flat, query_tr, query_add_tr, query_valid))
    return result.reshape(query_items, other_items)


def shards(encoded, slot_items, lengths, token_mask):
    n_enc = lax.axis_size("enc")
    n_pool = lax.axis_size("pool")
    owners = n_enc * n_pool
    group = encoded.shape[0]
    toks = encoded.shape[1]
    width = encoded.shape[2]
    items_dev = lengths.shape[0]
    per = items_dev // n_pool
    pool_index = lax.axis_index("pool")
    table = slot_items.reshape(owners, n_pool, per)
    mine = lax.dynamic_index_in_dim(table, pool_index, 1, keepdims=False) - pool_index * group
    outgoing = jnp.take(encoded, mine, axis=0)
    arrived = lax.all_to_all(outgoing, ("enc", "pool"), split_axis=0, concat_axis=0, tiled=True)
    arrived = arrived.reshape(n_enc, n_pool, per, toks, width)
    tok = n_enc * toks
    slotted = jnp.transpose(arrived, (1, 2, 0, 3, 4)).reshape(items_dev, tok, width)
    values = slotted.astype(jnp.float32)
    normed = (values / jnp.sqrt(jnp.sum(values * values, axis=-1, keepdims=True) + 1e-06)).astype(
        jnp.bfloat16
    )
    position = jnp.arange(tok, dtype=jnp.int32)[None, :]
    valid = (position < lengths[:, None]) & ((position == 0) | (token_mask == 1))
    bias = jnp.where(valid, 0.0, -4.0).astype(jnp.bfloat16).reshape(-1)
    block = normed.reshape(items_dev * tok, width)
    n_tok = items_dev * tok
    packed = jnp.concatenate([block, bias.reshape(-1, width)], axis=0)

    pool_index = lax.axis_index("pool")
    parity = (pool_index ^ (pool_index >> 1) ^ (pool_index >> 2)) & 1
    is_a = (pool_index & 1) == 0

    def par(p):
        return (p ^ (p >> 1) ^ (p >> 2)) & 1

    send_pairs = [(p, p ^ (4 if par(p) else 2)) for p in range(n_pool)]
    back_pairs = [(t, s) for s, t in send_pairs]
    chip_pairs = [(p, p ^ 1) for p in range(n_pool)]

    half = n_tok // 2
    first = jnp.concatenate([block[:half], bias.reshape(-1, width)], axis=0)
    z_first = lax.ppermute(first, "pool", send_pairs)
    z_second = lax.ppermute(block[half:], "pool", send_pairs)
    c_recv = lax.ppermute(packed, "pool", chip_pairs)

    c_blk, c_bias = c_recv[:n_tok], c_recv[n_tok:].reshape(-1)
    query = jnp.where(is_a, block[:half], c_blk[half:])
    query_bias = jnp.where(is_a, bias[:half], c_bias[half:])
    other = jnp.where(is_a, c_blk, block)
    other_bias = jnp.where(is_a, c_bias, bias)
    part = tile_scores(query, query_bias, other, other_bias, tok)
    part, z_first = lax.optimization_barrier((part, z_first))
    part_recv = lax.ppermute(part, "pool", chip_pairs)
    joined = jnp.where(
        is_a,
        jnp.concatenate([part, part_recv], axis=0),
        jnp.concatenate([part_recv, part], axis=0),
    )
    tile0 = jnp.where(is_a, joined, joined.T)

    z_bias = z_first[half:].reshape(-1)
    tile_a = tile_scores(block, bias, z_first[:half], z_bias[:half], tok)
    tile_a, z_second = lax.optimization_barrier((tile_a, z_second))
    back_a = lax.ppermute(tile_a.T, "pool", back_pairs)
    tile_b = tile_scores(block, bias, z_second, z_bias[half:], tok)
    back_b = lax.ppermute(tile_b.T, "pool", back_pairs)
    tile_z = jnp.concatenate([tile_a, tile_b], axis=1)
    tile_back = jnp.concatenate([back_a, back_b], axis=0)
    via_bit1 = parity == 1
    col1 = jnp.where(via_bit1, tile_z, tile_back)
    col2 = jnp.where(via_bit1, tile_back, tile_z)
    return jnp.concatenate([tile0, col1, col2], axis=1)


def solution(mesh):
    in_specs = (P("pool", "enc", None), P(), P(("enc", "pool")), P(("enc", "pool"), None))
    out_specs = P(("enc", "pool"), None)
    return jax.shard_map(shards, mesh=mesh, in_specs=in_specs, out_specs=out_specs, check_vma=False)
```

```python
import jax
import jax.numpy as jnp
from jax import lax
from jax.sharding import PartitionSpec as P


def from_partner(array, axis, stride):
    return lax.ppermute(array, axis, [(i, i ^ 1 << stride) for i in range(lax.axis_size(axis))])


def tile_scores(block, bias, other, other_bias, tok):
    query_items = block.shape[0] // tok
    other_items = other.shape[0] // tok
    width = block.shape[1]
    rows = min(32, query_items)
    blocks = query_items // rows
    other_tr = jnp.transpose(other.reshape(other_items, tok, width), (1, 0, 2))
    other_float = other_bias.astype(jnp.float32)
    other_add_tr = jnp.transpose(other_float.reshape(other_items, tok), (1, 0))[:, :, None]
    other_valid = (other_bias == 0).reshape(other_items, tok)
    query_flat = block.reshape(blocks, rows * tok, width)
    query_tr = jnp.transpose(block.reshape(blocks, rows, tok, width), (0, 2, 1, 3))
    bias_float = bias.astype(jnp.float32).reshape(blocks, rows, tok)
    query_add_tr = jnp.transpose(bias_float, (0, 2, 1))[..., None]
    query_valid = (bias == 0).reshape(blocks, rows, tok)

    def one_block(operands):
        flat, turned, adding, kept = operands
        dots_fore = jnp.einsum("ubh,qh->ubq", other_tr, flat, preferred_element_type=jnp.float32)
        fore = jnp.max(dots_fore + other_add_tr, axis=0).reshape(other_items, rows, tok)
        fore = jnp.sum(jnp.where(kept[None], fore, 0.0), axis=2)
        dots_back = jnp.einsum("trh,ch->trc", turned, other, preferred_element_type=jnp.float32)
        back = jnp.max(dots_back + adding, axis=0).reshape(rows, other_items, tok)
        back = jnp.sum(jnp.where(other_valid[None], back, 0.0), axis=2)
        return 0.5 * (fore.T + back)

    result = lax.map(one_block, (query_flat, query_tr, query_add_tr, query_valid))
    return result.reshape(query_items, other_items)


def shards(encoded, slot_items, lengths, token_mask):
    n_enc = lax.axis_size("enc")
    n_pool = lax.axis_size("pool")
    owners = n_enc * n_pool
    group = encoded.shape[0]
    toks = encoded.shape[1]
    width = encoded.shape[2]
    items_dev = lengths.shape[0]
    per = items_dev // n_pool
    pool_index = lax.axis_index("pool")
    table = slot_items.reshape(owners, n_pool, per)
    mine = lax.dynamic_index_in_dim(table, pool_index, 1, keepdims=False) - pool_index * group
    outgoing = jnp.take(encoded, mine, axis=0)
    arrived = lax.all_to_all(outgoing, ("enc", "pool"), split_axis=0, concat_axis=0, tiled=True)
    arrived = arrived.reshape(n_enc, n_pool, per, toks, width)
    tok = n_enc * toks
    slotted = jnp.transpose(arrived, (1, 2, 0, 3, 4)).reshape(items_dev, tok, width)
    values = slotted.astype(jnp.float32)
    normed = (values / jnp.sqrt(jnp.sum(values * values, axis=-1, keepdims=True) + 1e-06)).astype(
        jnp.bfloat16
    )
    position = jnp.arange(tok, dtype=jnp.int32)[None, :]
    valid = (position < lengths[:, None]) & ((position == 0) | (token_mask == 1))
    bias = jnp.where(valid, 0.0, -4.0).astype(jnp.bfloat16).reshape(-1)
    block = normed.reshape(items_dev * tok, width)
    n_tok = items_dev * tok
    packed = jnp.concatenate([block, bias.reshape(-1, width)], axis=0)

    pool_index = lax.axis_index("pool")
    parity = (pool_index ^ (pool_index >> 1) ^ (pool_index >> 2)) & 1
    is_a = (pool_index & 1) == 0

    def par(p):
        return (p ^ (p >> 1) ^ (p >> 2)) & 1

    send_pairs = [(p, p ^ (4 if par(p) else 2)) for p in range(n_pool)]
    back_pairs = [(t, s) for s, t in send_pairs]
    chip_pairs = [(p, p ^ 1) for p in range(n_pool)]

    half = n_tok // 2
    bias_rows = half // width
    pad_rows = -bias_rows % 16
    pad = jnp.zeros((pad_rows, width), jnp.bfloat16)
    first = jnp.concatenate([block[:half], bias[:half].reshape(bias_rows, width), pad], axis=0)
    second = jnp.concatenate([block[half:], bias[half:].reshape(bias_rows, width), pad], axis=0)
    z_first = lax.ppermute(first, "pool", send_pairs)
    c_recv = lax.ppermute(packed, "pool", chip_pairs)

    c_blk, c_bias = c_recv[:n_tok], c_recv[n_tok:].reshape(-1)
    query = jnp.where(is_a, block[:half], c_blk[half:])
    query_bias = jnp.where(is_a, bias[:half], c_bias[half:])
    other = jnp.where(is_a, c_blk, block)
    other_bias = jnp.where(is_a, c_bias, bias)
    part = tile_scores(query, query_bias, other, other_bias, tok)
    part, z_first = lax.optimization_barrier((part, z_first))
    part_recv = lax.ppermute(part, "pool", chip_pairs)
    joined = jnp.where(
        is_a,
        jnp.concatenate([part, part_recv], axis=0),
        jnp.concatenate([part_recv, part], axis=0),
    )
    tile0 = jnp.where(is_a, joined, joined.T)

    second, z_first = lax.optimization_barrier((second, z_first))
    z_second = lax.ppermute(second, "pool", send_pairs)
    tile_a = tile_scores(block, bias, z_first[:half], z_first[half:half + bias_rows].reshape(-1), tok)
    tile_a, z_second = lax.optimization_barrier((tile_a, z_second))
    back_a = lax.ppermute(tile_a.T, "pool", back_pairs)
    tile_b = tile_scores(block, bias, z_second[:half], z_second[half:half + bias_rows].reshape(-1), tok)
    back_b = lax.ppermute(tile_b.T, "pool", back_pairs)
    tile_z = jnp.concatenate([tile_a, tile_b], axis=1)
    tile_back = jnp.concatenate([back_a, back_b], axis=0)
    via_bit1 = parity == 1
    col1 = jnp.where(via_bit1, tile_z, tile_back)
    col2 = jnp.where(via_bit1, tile_back, tile_z)
    return jnp.concatenate([tile0, col1, col2], axis=1)


def solution(mesh):
    in_specs = (P("pool", "enc", None), P(), P(("enc", "pool")), P(("enc", "pool"), None))
    out_specs = P(("enc", "pool"), None)
    return jax.shard_map(shards, mesh=mesh, in_specs=in_specs, out_specs=out_specs, check_vma=False)
```

```python
import jax
import jax.numpy as jnp
from jax import lax
from jax.sharding import PartitionSpec as P


def from_partner(array, axis, stride):
    return lax.ppermute(array, axis, [(i, i ^ 1 << stride) for i in range(lax.axis_size(axis))])


def tile_scores(block, bias, other, other_bias, tok):
    query_items = block.shape[0] // tok
    other_items = other.shape[0] // tok
    width = block.shape[1]
    rows = min(32, query_items)
    blocks = query_items // rows
    other_tr = jnp.transpose(other.reshape(other_items, tok, width), (1, 0, 2))
    other_float = other_bias.astype(jnp.float32)
    other_add_tr = jnp.transpose(other_float.reshape(other_items, tok), (1, 0))[:, :, None]
    other_valid = (other_bias == 0).reshape(other_items, tok)
    query_flat = block.reshape(blocks, rows * tok, width)
    query_tr = jnp.transpose(block.reshape(blocks, rows, tok, width), (0, 2, 1, 3))
    bias_float = bias.astype(jnp.float32).reshape(blocks, rows, tok)
    query_add_tr = jnp.transpose(bias_float, (0, 2, 1))[..., None]
    query_valid = (bias == 0).reshape(blocks, rows, tok)

    def one_block(operands):
        flat, turned, adding, kept = operands
        dots_fore = jnp.einsum("ubh,qh->ubq", other_tr, flat, preferred_element_type=jnp.float32)
        fore = jnp.max(dots_fore + other_add_tr, axis=0).reshape(other_items, rows, tok)
        fore = jnp.sum(jnp.where(kept[None], fore, 0.0), axis=2)
        dots_back = jnp.einsum("trh,ch->trc", turned, other, preferred_element_type=jnp.float32)
        back = jnp.max(dots_back + adding, axis=0).reshape(rows, other_items, tok)
        back = jnp.sum(jnp.where(other_valid[None], back, 0.0), axis=2)
        return 0.5 * (fore.T + back)

    result = lax.map(one_block, (query_flat, query_tr, query_add_tr, query_valid))
    return result.reshape(query_items, other_items)


def shards(encoded, slot_items, lengths, token_mask):
    n_enc = lax.axis_size("enc")
    n_pool = lax.axis_size("pool")
    owners = n_enc * n_pool
    group = encoded.shape[0]
    toks = encoded.shape[1]
    width = encoded.shape[2]
    items_dev = lengths.shape[0]
    per = items_dev // n_pool
    pool_index = lax.axis_index("pool")
    slot_of = (jnp.arange(owners, dtype=jnp.int32) * items_dev + pool_index * per)[:, None] + jnp.arange(
        per, dtype=jnp.int32
    )[None, :]
    mine = jnp.take(slot_items, slot_of, mode="clip") - pool_index * group
    outgoing = jnp.take(encoded, mine, axis=0, mode="clip")
    arrived = lax.all_to_all(outgoing, ("enc", "pool"), split_axis=0, concat_axis=0, tiled=True)
    arrived = arrived.reshape(n_enc, n_pool, per, toks, width)
    tok = n_enc * toks
    slotted = jnp.transpose(arrived, (1, 2, 0, 3, 4)).reshape(items_dev, tok, width)
    values = slotted.astype(jnp.float32)
    normed = (values / jnp.sqrt(jnp.sum(values * values, axis=-1, keepdims=True) + 1e-06)).astype(
        jnp.bfloat16
    )
    position = jnp.arange(tok, dtype=jnp.int32)[None, :]
    valid = (position < lengths[:, None]) & ((position == 0) | (token_mask == 1))
    bias = jnp.where(valid, 0.0, -4.0).astype(jnp.bfloat16).reshape(-1)
    n_tok = items_dev * tok
    packed = jnp.concatenate([normed.reshape(n_tok, width), bias.reshape(-1, width)], axis=0)
    block = packed[:n_tok]

    pool_index = lax.axis_index("pool")
    parity = (pool_index ^ (pool_index >> 1) ^ (pool_index >> 2)) & 1
    is_a = (pool_index & 1) == 0

    def par(p):
        return (p ^ (p >> 1) ^ (p >> 2)) & 1

    send_pairs = [(p, p ^ (4 if par(p) else 2)) for p in range(n_pool)]
    back_pairs = [(t, s) for s, t in send_pairs]
    chip_pairs = [(p, p ^ 1) for p in range(n_pool)]

    z_recv = lax.ppermute(packed, "pool", send_pairs)
    c_recv = lax.ppermute(packed, "pool", chip_pairs)

    half = n_tok // 2
    c_blk, c_bias = c_recv[:n_tok], c_recv[n_tok:].reshape(-1)
    query = jnp.where(is_a, block[:half], c_blk[half:])
    query_bias = jnp.where(is_a, bias[:half], c_bias[half:])
    other = jnp.where(is_a, c_blk, block)
    other_bias = jnp.where(is_a, c_bias, bias)
    part = tile_scores(query, query_bias, other, other_bias, tok)
    part_recv = lax.ppermute(part, "pool", chip_pairs)
    joined = jnp.where(
        is_a,
        jnp.concatenate([part, part_recv], axis=0),
        jnp.concatenate([part_recv, part], axis=0),
    )
    tile0 = jnp.where(is_a, joined, joined.T)

    z_blk, z_bias = z_recv[:n_tok], z_recv[n_tok:].reshape(-1)
    tile_z = tile_scores(block, bias, z_blk, z_bias, tok)
    tile_back = lax.ppermute(tile_z.T, "pool", back_pairs)
    via_bit1 = parity == 1
    col1 = jnp.where(via_bit1, tile_z, tile_back)
    col2 = jnp.where(via_bit1, tile_back, tile_z)
    return jnp.concatenate([tile0, col1, col2], axis=1)


def solution(mesh):
    in_specs = (P("pool", "enc", None), P(), P(("enc", "pool")), P(("enc", "pool"), None))
    out_specs = P(("enc", "pool"), None)
    return jax.shard_map(shards, mesh=mesh, in_specs=in_specs, out_specs=out_specs, check_vma=False)
```

```python
import jax
import jax.numpy as jnp
from jax import lax
from jax.sharding import PartitionSpec as P


def tile_scores(query, query_bias, other, other_bias):
    tok, query_items, width = query.shape
    other_items = other.shape[1]
    rows = min(32, query_items)
    blocks = query_items // rows
    other_flat = other.reshape(tok * other_items, width)
    other_add = other_bias.astype(jnp.float32)[:, :, None]
    other_valid = other_bias == 0
    turned_all = jnp.transpose(query.reshape(tok, blocks, rows, width), (1, 0, 2, 3))
    adding_all = jnp.transpose(query_bias.astype(jnp.float32).reshape(tok, blocks, rows), (1, 0, 2))[..., None]
    kept_all = jnp.transpose((query_bias == 0).reshape(tok, blocks, rows), (1, 0, 2))

    def one_block(operands):
        turned, adding, kept = operands
        flat = turned.reshape(tok * rows, width)
        dots_fore = jnp.einsum("ubh,qh->ubq", other, flat, preferred_element_type=jnp.float32)
        fore = jnp.max(dots_fore + other_add, axis=0).reshape(other_items, tok, rows)
        fore = jnp.sum(jnp.where(kept[None], fore, 0.0), axis=1)
        dots_back = jnp.einsum("trh,ch->trc", turned, other_flat, preferred_element_type=jnp.float32)
        back = jnp.max(dots_back + adding, axis=0).reshape(rows, tok, other_items)
        back = jnp.sum(jnp.where(other_valid[None], back, 0.0), axis=1)
        return 0.5 * (fore.T + back)

    result = lax.map(one_block, (turned_all, adding_all, kept_all))
    return result.reshape(query_items, other_items)


def shards(encoded, slot_items, lengths, token_mask):
    n_enc = lax.axis_size("enc")
    n_pool = lax.axis_size("pool")
    owners = n_enc * n_pool
    group = encoded.shape[0]
    toks = encoded.shape[1]
    width = encoded.shape[2]
    items_dev = lengths.shape[0]
    per = items_dev // n_pool
    tok = n_enc * toks
    n_tok = items_dev * tok
    pool_index = lax.axis_index("pool")

    table = slot_items.reshape(owners, n_pool, per)
    mine = lax.dynamic_index_in_dim(table, pool_index, 1, keepdims=False) - pool_index * group
    outgoing = jnp.take(encoded, mine, axis=0, mode="clip")
    outgoing = jnp.transpose(outgoing, (2, 0, 1, 3))
    arrived = lax.all_to_all(outgoing, ("enc", "pool"), split_axis=1, concat_axis=1, tiled=True)
    slotted = arrived.reshape(tok, items_dev, width)
    values = slotted.astype(jnp.float32)
    normed = (values / jnp.sqrt(jnp.sum(values * values, axis=-1, keepdims=True) + 1e-06)).astype(
        jnp.bfloat16
    )
    position = jnp.arange(tok, dtype=jnp.int32)[None, :]
    valid = (position < lengths[:, None]) & ((position == 0) | (token_mask == 1))
    valid_tm = jnp.transpose(valid.reshape(items_dev, n_enc, toks), (2, 1, 0)).reshape(tok, items_dev)
    bias = jnp.where(valid_tm, 0.0, -4.0).astype(jnp.bfloat16)
    packed = jnp.concatenate([normed.reshape(n_tok, width), bias.reshape(-1, width)], axis=0)
    block = packed[:n_tok].reshape(tok, items_dev, width)

    parity = (pool_index ^ (pool_index >> 1) ^ (pool_index >> 2)) & 1
    is_a = (pool_index & 1) == 0

    def par(p):
        return (p ^ (p >> 1) ^ (p >> 2)) & 1

    send_pairs = [(p, p ^ (4 if par(p) else 2)) for p in range(n_pool)]
    back_pairs = [(t, s) for s, t in send_pairs]
    chip_pairs = [(p, p ^ 1) for p in range(n_pool)]

    z_recv = lax.ppermute(packed, "pool", send_pairs)
    c_recv = lax.ppermute(packed, "pool", chip_pairs)

    def unpack(received):
        return received[:n_tok].reshape(tok, items_dev, width), received[n_tok:].reshape(tok, items_dev)

    half = items_dev // 2
    c_blk, c_bias = unpack(c_recv)
    query = jnp.where(is_a, block[:, :half], c_blk[:, half:])
    query_bias = jnp.where(is_a, bias[:, :half], c_bias[:, half:])
    other = jnp.where(is_a, c_blk, block)
    other_bias = jnp.where(is_a, c_bias, bias)
    part = tile_scores(query, query_bias, other, other_bias)
    part_recv = lax.ppermute(part, "pool", chip_pairs)
    joined = jnp.where(
        is_a,
        jnp.concatenate([part, part_recv], axis=0),
        jnp.concatenate([part_recv, part], axis=0),
    )
    tile0 = jnp.where(is_a, joined, joined.T)

    z_blk, z_bias = unpack(z_recv)
    tile_z = tile_scores(block, bias, z_blk, z_bias)
    tile_back = lax.ppermute(tile_z.T, "pool", back_pairs)
    via_bit1 = parity == 1
    col1 = jnp.where(via_bit1, tile_z, tile_back)
    col2 = jnp.where(via_bit1, tile_back, tile_z)
    return jnp.concatenate([tile0, col1, col2], axis=1)


def solution(mesh):
    in_specs = (P("pool", "enc", None), P(), P(("enc", "pool")), P(("enc", "pool"), None))
    out_specs = P(("enc", "pool"), None)
    return jax.shard_map(shards, mesh=mesh, in_specs=in_specs, out_specs=out_specs, check_vma=False)
```

```python
import jax
import jax.numpy as jnp
from jax import lax
from jax.sharding import PartitionSpec as P


def tile_scores(query, query_bias, other, other_bias):
    tok, query_items, width = query.shape
    other_items = other.shape[1]
    rows = min(32, query_items)
    blocks = query_items // rows
    other_flat = other.reshape(tok * other_items, width)
    other_valid = other_bias == 0
    turned_all = jnp.transpose(query.reshape(tok, blocks, rows, width), (1, 0, 2, 3))
    kept_all = jnp.transpose((query_bias == 0).reshape(tok, blocks, rows), (1, 0, 2))

    def one_block(operands):
        turned, kept = operands
        flat = turned.reshape(tok * rows, width)
        dots_fore = jnp.einsum("ubh,qh->ubq", other, flat, preferred_element_type=jnp.float32)
        fore = jnp.max(dots_fore, axis=0).reshape(other_items, tok, rows)
        fore = jnp.sum(jnp.where(kept[None], fore, 0.0), axis=1)
        dots_back = jnp.einsum("trh,ch->trc", turned, other_flat, preferred_element_type=jnp.float32)
        back = jnp.max(dots_back, axis=0).reshape(rows, tok, other_items)
        back = jnp.sum(jnp.where(other_valid[None], back, 0.0), axis=1)
        return 0.5 * (fore.T + back)

    result = lax.map(one_block, (turned_all, kept_all))
    return result.reshape(query_items, other_items)


def shards(encoded, slot_items, lengths, token_mask):
    n_enc = lax.axis_size("enc")
    n_pool = lax.axis_size("pool")
    owners = n_enc * n_pool
    group = encoded.shape[0]
    toks = encoded.shape[1]
    width = encoded.shape[2]
    items_dev = lengths.shape[0]
    per = items_dev // n_pool
    tok = n_enc * toks
    n_tok = items_dev * tok
    pool_index = lax.axis_index("pool")

    table = slot_items.reshape(owners, n_pool, per)
    mine = lax.dynamic_index_in_dim(table, pool_index, 1, keepdims=False) - pool_index * group
    dnums = lax.GatherDimensionNumbers(offset_dims=(0, 3), collapsed_slice_dims=(0,), start_index_map=(0,))
    outgoing = lax.gather(
        encoded, mine[..., None], dnums, (1, toks, width), mode=lax.GatherScatterMode.CLIP
    )
    arrived = lax.all_to_all(outgoing, ("enc", "pool"), split_axis=1, concat_axis=1, tiled=True)
    slotted = arrived.reshape(tok, items_dev, width)
    position = jnp.arange(tok, dtype=jnp.int32)[None, :]
    valid = (position < lengths[:, None]) & ((position == 0) | (token_mask == 1))
    valid_tm = jnp.transpose(valid.reshape(items_dev, n_enc, toks), (2, 1, 0)).reshape(tok, items_dev)
    bias = jnp.where(valid_tm, 0.0, -4.0).astype(jnp.bfloat16)
    values = slotted.astype(jnp.float32)
    normed = (values / jnp.sqrt(jnp.sum(values * values, axis=-1, keepdims=True) + 1e-06)).astype(
        jnp.bfloat16
    )
    normed = jnp.where(valid_tm[:, :, None], normed, normed[0][None])
    packed = jnp.concatenate([normed.reshape(n_tok, width), bias.reshape(-1, width)], axis=0)
    block = packed[:n_tok].reshape(tok, items_dev, width)

    parity = (pool_index ^ (pool_index >> 1) ^ (pool_index >> 2)) & 1
    is_a = (pool_index & 1) == 0

    def par(p):
        return (p ^ (p >> 1) ^ (p >> 2)) & 1

    send_pairs = [(p, p ^ (4 if par(p) else 2)) for p in range(n_pool)]
    back_pairs = [(t, s) for s, t in send_pairs]
    chip_pairs = [(p, p ^ 1) for p in range(n_pool)]

    z_recv = lax.ppermute(packed, "pool", send_pairs)
    c_recv = lax.ppermute(packed, "pool", chip_pairs)

    def unpack(received):
        return received[:n_tok].reshape(tok, items_dev, width), received[n_tok:].reshape(tok, items_dev)

    half = items_dev // 2
    c_blk, c_bias = unpack(c_recv)
    query = jnp.where(is_a, block[:, :half], c_blk[:, half:])
    query_bias = jnp.where(is_a, bias[:, :half], c_bias[:, half:])
    other = jnp.where(is_a, c_blk, block)
    other_bias = jnp.where(is_a, c_bias, bias)
    part = tile_scores(query, query_bias, other, other_bias)
    part_recv = lax.ppermute(part, "pool", chip_pairs)
    joined = jnp.where(
        is_a,
        jnp.concatenate([part, part_recv], axis=0),
        jnp.concatenate([part_recv, part], axis=0),
    )
    tile0 = jnp.where(is_a, joined, joined.T)

    z_blk, z_bias = unpack(z_recv)
    tile_z = tile_scores(block, bias, z_blk, z_bias)
    tile_back = lax.ppermute(tile_z.T, "pool", back_pairs)
    via_bit1 = parity == 1
    col1 = jnp.where(via_bit1, tile_z, tile_back)
    col2 = jnp.where(via_bit1, tile_back, tile_z)
    return jnp.concatenate([tile0, col1, col2], axis=1)


def solution(mesh):
    in_specs = (P("pool", "enc", None), P(), P(("enc", "pool")), P(("enc", "pool"), None))
    out_specs = P(("enc", "pool"), None)
    return jax.shard_map(shards, mesh=mesh, in_specs=in_specs, out_specs=out_specs, check_vma=False)
```

```python
import jax
import jax.numpy as jnp
from jax import lax
from jax.sharding import PartitionSpec as P


def tile_scores(query, query_bias, other, other_bias):
    tok, query_items, width = query.shape
    other_items = other.shape[1]
    rows = min(32, query_items)
    blocks = query_items // rows
    other_flat = other.reshape(tok * other_items, width)
    other_add = other_bias.astype(jnp.float32)[:, :, None]
    other_valid = other_bias == 0
    turned_all = jnp.transpose(query.reshape(tok, blocks, rows, width), (1, 0, 2, 3))
    adding_all = jnp.transpose(query_bias.astype(jnp.float32).reshape(tok, blocks, rows), (1, 0, 2))[..., None]
    kept_all = jnp.transpose((query_bias == 0).reshape(tok, blocks, rows), (1, 0, 2))

    def one_block(operands):
        turned, adding, kept = operands
        flat = turned.reshape(tok * rows, width)
        dots_fore = jnp.einsum("ubh,qh->ubq", other, flat, preferred_element_type=jnp.float32)
        fore = jnp.max(dots_fore + other_add, axis=0).reshape(other_items, tok, rows)
        fore = jnp.sum(jnp.where(kept[None], fore, 0.0), axis=1)
        dots_back = jnp.einsum("trh,ch->trc", turned, other_flat, preferred_element_type=jnp.float32)
        back = jnp.max(dots_back + adding, axis=0).reshape(rows, tok, other_items)
        back = jnp.sum(jnp.where(other_valid[None], back, 0.0), axis=1)
        return 0.5 * (fore.T + back)

    result = lax.map(one_block, (turned_all, adding_all, kept_all))
    return result.reshape(query_items, other_items)


def shards(encoded, slot_items, lengths, token_mask):
    n_enc = lax.axis_size("enc")
    n_pool = lax.axis_size("pool")
    owners = n_enc * n_pool
    group = encoded.shape[0]
    toks = encoded.shape[1]
    width = encoded.shape[2]
    items_dev = lengths.shape[0]
    per = items_dev // n_pool
    tok = n_enc * toks
    n_tok = items_dev * tok
    pool_index = lax.axis_index("pool")

    lanes = 128
    if lanes % items_dev == 0 and slot_items.shape[0] % lanes == 0:
        per_row = lanes // items_dev
        view = slot_items.reshape(-1, lanes)
        pieces = [
            lax.dynamic_slice_in_dim(view, h * items_dev + pool_index * per, per, axis=1) for h in range(per_row)
        ]
        table = jnp.concatenate(pieces, axis=1).reshape(owners, per)
    else:
        table = lax.dynamic_index_in_dim(slot_items.reshape(owners, n_pool, per), pool_index, 1, keepdims=False)
    mine = table - pool_index * group
    outgoing = jnp.take(encoded, mine, axis=0, mode="clip")
    outgoing = jnp.transpose(outgoing, (2, 0, 1, 3))
    arrived = lax.all_to_all(outgoing, ("enc", "pool"), split_axis=1, concat_axis=1, tiled=True)
    slotted = arrived.reshape(tok, items_dev, width)
    values = slotted.astype(jnp.float32)
    normed = (values / jnp.sqrt(jnp.sum(values * values, axis=-1, keepdims=True) + 1e-06)).astype(
        jnp.bfloat16
    )
    position = jnp.arange(tok, dtype=jnp.int32)[None, :]
    valid = (position < lengths[:, None]) & ((position == 0) | (token_mask == 1))
    valid_tm = jnp.transpose(valid.reshape(items_dev, n_enc, toks), (2, 1, 0)).reshape(tok, items_dev)
    bias = jnp.where(valid_tm, 0.0, -4.0).astype(jnp.bfloat16)
    packed = jnp.concatenate([normed.reshape(n_tok, width), bias.reshape(-1, width)], axis=0)
    block = packed[:n_tok].reshape(tok, items_dev, width)

    parity = (pool_index ^ (pool_index >> 1) ^ (pool_index >> 2)) & 1
    is_a = (pool_index & 1) == 0

    def par(p):
        return (p ^ (p >> 1) ^ (p >> 2)) & 1

    send_pairs = [(p, p ^ (4 if par(p) else 2)) for p in range(n_pool)]
    back_pairs = [(t, s) for s, t in send_pairs]
    chip_pairs = [(p, p ^ 1) for p in range(n_pool)]

    z_recv = lax.ppermute(packed, "pool", send_pairs)
    c_recv = lax.ppermute(packed, "pool", chip_pairs)

    def unpack(received):
        return received[:n_tok].reshape(tok, items_dev, width), received[n_tok:].reshape(tok, items_dev)

    half = items_dev // 2
    c_blk, c_bias = unpack(c_recv)
    query = jnp.where(is_a, block[:, :half], c_blk[:, half:])
    query_bias = jnp.where(is_a, bias[:, :half], c_bias[:, half:])
    other = jnp.where(is_a, c_blk, block)
    other_bias = jnp.where(is_a, c_bias, bias)
    part = tile_scores(query, query_bias, other, other_bias)
    part_recv = lax.ppermute(part, "pool", chip_pairs)
    joined = jnp.where(
        is_a,
        jnp.concatenate([part, part_recv], axis=0),
        jnp.concatenate([part_recv, part], axis=0),
    )
    tile0 = jnp.where(is_a, joined, joined.T)

    z_blk, z_bias = unpack(z_recv)
    tile_z = tile_scores(block, bias, z_blk, z_bias)
    tile_back = lax.ppermute(tile_z.T, "pool", back_pairs)
    via_bit1 = parity == 1
    col1 = jnp.where(via_bit1, tile_z, tile_back)
    col2 = jnp.where(via_bit1, tile_back, tile_z)
    return jnp.concatenate([tile0, col1, col2], axis=1)


def solution(mesh):
    in_specs = (P("pool", "enc", None), P(), P(("enc", "pool")), P(("enc", "pool"), None))
    out_specs = P(("enc", "pool"), None)
    return jax.shard_map(shards, mesh=mesh, in_specs=in_specs, out_specs=out_specs, check_vma=False)
```

```python
import jax
import jax.numpy as jnp
from jax import lax
from jax.sharding import PartitionSpec as P


def tile_scores(query, query_bias, other, other_bias):
    tok, query_items, width = query.shape
    other_items = other.shape[1]
    rows = min(64, query_items)
    blocks = query_items // rows
    other_flat = other.reshape(tok * other_items, width)
    other_add = other_bias.astype(jnp.float32)[:, :, None]
    other_valid = other_bias == 0
    turned_all = jnp.transpose(query.reshape(tok, blocks, rows, width), (1, 0, 2, 3))
    adding_all = jnp.transpose(query_bias.astype(jnp.float32).reshape(tok, blocks, rows), (1, 0, 2))[..., None]
    kept_all = jnp.transpose((query_bias == 0).reshape(tok, blocks, rows), (1, 0, 2))

    def one_block(operands):
        turned, adding, kept = operands
        flat = turned.reshape(tok * rows, width)
        dots_fore = jnp.einsum("ubh,qh->ubq", other, flat, preferred_element_type=jnp.float32)
        fore = jnp.max(dots_fore + other_add, axis=0).reshape(other_items, tok, rows)
        fore = jnp.sum(jnp.where(kept[None], fore, 0.0), axis=1)
        dots_back = jnp.einsum("trh,ch->trc", turned, other_flat, preferred_element_type=jnp.float32)
        back = jnp.max(dots_back + adding, axis=0).reshape(rows, tok, other_items)
        back = jnp.sum(jnp.where(other_valid[None], back, 0.0), axis=1)
        return 0.5 * (fore.T + back)

    result = lax.map(one_block, (turned_all, adding_all, kept_all))
    return result.reshape(query_items, other_items)


def shards(encoded, slot_items, lengths, token_mask):
    n_enc = lax.axis_size("enc")
    n_pool = lax.axis_size("pool")
    owners = n_enc * n_pool
    group = encoded.shape[0]
    toks = encoded.shape[1]
    width = encoded.shape[2]
    items_dev = lengths.shape[0]
    per = items_dev // n_pool
    tok = n_enc * toks
    n_tok = items_dev * tok
    pool_index = lax.axis_index("pool")

    table = slot_items.reshape(owners, n_pool, per)
    mine = lax.dynamic_index_in_dim(table, pool_index, 1, keepdims=False) - pool_index * group
    outgoing = jnp.take(encoded, mine, axis=0, mode="clip")
    outgoing = jnp.transpose(outgoing, (2, 0, 1, 3))
    arrived = lax.all_to_all(outgoing, ("enc", "pool"), split_axis=1, concat_axis=1, tiled=True)
    slotted = arrived.reshape(tok, items_dev, width)
    values = slotted.astype(jnp.float32)
    normed = (values / jnp.sqrt(jnp.sum(values * values, axis=-1, keepdims=True) + 1e-06)).astype(
        jnp.bfloat16
    )
    position = jnp.arange(tok, dtype=jnp.int32)[None, :]
    valid = (position < lengths[:, None]) & ((position == 0) | (token_mask == 1))
    valid_tm = jnp.transpose(valid.reshape(items_dev, n_enc, toks), (2, 1, 0)).reshape(tok, items_dev)
    bias = jnp.where(valid_tm, 0.0, -4.0).astype(jnp.bfloat16)
    packed = jnp.concatenate([normed.reshape(n_tok, width), bias.reshape(-1, width)], axis=0)
    block = packed[:n_tok].reshape(tok, items_dev, width)

    parity = (pool_index ^ (pool_index >> 1) ^ (pool_index >> 2)) & 1
    is_a = (pool_index & 1) == 0

    def par(p):
        return (p ^ (p >> 1) ^ (p >> 2)) & 1

    send_pairs = [(p, p ^ (4 if par(p) else 2)) for p in range(n_pool)]
    back_pairs = [(t, s) for s, t in send_pairs]
    chip_pairs = [(p, p ^ 1) for p in range(n_pool)]

    z_recv = lax.ppermute(packed, "pool", send_pairs)
    c_recv = lax.ppermute(packed, "pool", chip_pairs)

    def unpack(received):
        return received[:n_tok].reshape(tok, items_dev, width), received[n_tok:].reshape(tok, items_dev)

    half = items_dev // 2
    c_blk, c_bias = unpack(c_recv)
    query = jnp.where(is_a, block[:, :half], c_blk[:, half:])
    query_bias = jnp.where(is_a, bias[:, :half], c_bias[:, half:])
    other = jnp.where(is_a, c_blk, block)
    other_bias = jnp.where(is_a, c_bias, bias)
    part = tile_scores(query, query_bias, other, other_bias)
    part_recv = lax.ppermute(part, "pool", chip_pairs)
    joined = jnp.where(
        is_a,
        jnp.concatenate([part, part_recv], axis=0),
        jnp.concatenate([part_recv, part], axis=0),
    )
    tile0 = jnp.where(is_a, joined, joined.T)

    z_blk, z_bias = unpack(z_recv)
    tile_z = tile_scores(block, bias, z_blk, z_bias)
    tile_back = lax.ppermute(tile_z.T, "pool", back_pairs)
    via_bit1 = parity == 1
    col1 = jnp.where(via_bit1, tile_z, tile_back)
    col2 = jnp.where(via_bit1, tile_back, tile_z)
    return jnp.concatenate([tile0, col1, col2], axis=1)


def solution(mesh):
    in_specs = (P("pool", "enc", None), P(), P(("enc", "pool")), P(("enc", "pool"), None))
    out_specs = P(("enc", "pool"), None)
    return jax.shard_map(shards, mesh=mesh, in_specs=in_specs, out_specs=out_specs, check_vma=False)
```

```python
import jax
import jax.numpy as jnp
from jax import lax
from jax.sharding import PartitionSpec as P


def tile_scores(query, query_bias, other, other_bias):
    tok, query_items, width = query.shape
    other_items = other.shape[1]
    rows = min(32, query_items)
    blocks = query_items // rows
    other_flat = other.reshape(tok * other_items, width)
    other_add = other_bias.astype(jnp.float32)[:, :, None]
    other_valid = other_bias == 0
    turned_all = jnp.transpose(query.reshape(tok, blocks, rows, width), (1, 0, 2, 3))
    adding_all = jnp.transpose(query_bias.astype(jnp.float32).reshape(tok, blocks, rows), (1, 0, 2))[..., None]
    kept_all = jnp.transpose((query_bias == 0).reshape(tok, blocks, rows), (1, 0, 2))

    def one_block(operands):
        turned, adding, kept = operands
        flat = turned.reshape(tok * rows, width)
        dots_fore = jnp.einsum("ubh,qh->ubq", other, flat, preferred_element_type=jnp.float32)
        fore = jnp.max(dots_fore + other_add, axis=0).reshape(other_items, tok, rows)
        fore = jnp.sum(jnp.where(kept[None], fore, 0.0), axis=1)
        dots_back = jnp.einsum("trh,ch->trc", turned, other_flat, preferred_element_type=jnp.float32)
        back = jnp.max(dots_back + adding, axis=0).reshape(rows, tok, other_items)
        back = jnp.sum(jnp.where(other_valid[None], back, 0.0), axis=1)
        return 0.5 * (fore.T + back)

    result = lax.map(one_block, (turned_all, adding_all, kept_all))
    return result.reshape(query_items, other_items)


def shards(encoded, slot_items, lengths, token_mask):
    n_enc = lax.axis_size("enc")
    n_pool = lax.axis_size("pool")
    owners = n_enc * n_pool
    group = encoded.shape[0]
    toks = encoded.shape[1]
    width = encoded.shape[2]
    items_dev = lengths.shape[0]
    per = items_dev // n_pool
    tok = n_enc * toks
    n_tok = items_dev * tok
    pool_index = lax.axis_index("pool")

    table = slot_items.reshape(owners, n_pool, per)
    mine = lax.dynamic_index_in_dim(table, pool_index, 1, keepdims=False) - pool_index * group
    outgoing = jnp.take(encoded, mine, axis=0, mode="clip")
    outgoing = jnp.transpose(outgoing, (2, 0, 1, 3))
    arrived = lax.all_to_all(outgoing, ("enc", "pool"), split_axis=1, concat_axis=1, tiled=True)
    slotted = arrived.reshape(tok, items_dev, width)
    values = slotted.astype(jnp.float32)
    normed = (values / jnp.sqrt(jnp.sum(values * values, axis=-1, keepdims=True) + 1e-06)).astype(
        jnp.bfloat16
    )
    position = jnp.arange(tok, dtype=jnp.int32)[None, :]
    valid = (position < lengths[:, None]) & ((position == 0) | (token_mask == 1))
    valid_tm = jnp.transpose(valid.reshape(items_dev, n_enc, toks), (2, 1, 0)).reshape(tok, items_dev)
    bias = jnp.where(valid_tm, 0.0, -4.0).astype(jnp.bfloat16)
    packed = jnp.concatenate([normed.reshape(n_tok, width), bias.reshape(-1, width)], axis=0)
    block = packed[:n_tok].reshape(tok, items_dev, width)

    parity = (pool_index ^ (pool_index >> 1) ^ (pool_index >> 2)) & 1
    is_a = (pool_index & 1) == 0

    def par(p):
        return (p ^ (p >> 1) ^ (p >> 2)) & 1

    send_pairs = [(p, p ^ (4 if par(p) else 2)) for p in range(n_pool)]
    back_pairs = [(t, s) for s, t in send_pairs]
    chip_pairs = [(p, p ^ 1) for p in range(n_pool)]

    z_recv = lax.ppermute(packed, "pool", send_pairs)
    c_recv = lax.ppermute(packed, "pool", chip_pairs)

    def unpack(received):
        return received[:n_tok].reshape(tok, items_dev, width), received[n_tok:].reshape(tok, items_dev)

    half = items_dev // 2
    c_blk, c_bias = unpack(c_recv)
    query = jnp.where(is_a, block[:, :half], c_blk[:, half:])
    query_bias = jnp.where(is_a, bias[:, :half], c_bias[:, half:])
    other = jnp.where(is_a, c_blk, block)
    other_bias = jnp.where(is_a, c_bias, bias)
    part = tile_scores(query, query_bias, other, other_bias)
    part_recv = lax.ppermute(part, "pool", chip_pairs)
    joined = jnp.where(
        is_a,
        jnp.concatenate([part, part_recv], axis=0),
        jnp.concatenate([part_recv, part], axis=0),
    )
    tile0 = jnp.where(is_a, joined, joined.T)

    z_blk, z_bias = unpack(z_recv)
    tile_z = tile_scores(block, bias, z_blk, z_bias)
    tile_back = lax.ppermute(tile_z.T, "pool", back_pairs)
    other_items = tile_z.shape[1]
    z_col = (2 - parity) * other_items
    back_col = (1 + parity) * other_items
    scores = jnp.zeros((items_dev, 3 * other_items), jnp.float32)
    scores = lax.dynamic_update_slice_in_dim(scores, tile0, 0, axis=1)
    scores = lax.dynamic_update_slice_in_dim(scores, tile_z, z_col, axis=1)
    return lax.dynamic_update_slice_in_dim(scores, tile_back, back_col, axis=1)


def solution(mesh):
    in_specs = (P("pool", "enc", None), P(), P(("enc", "pool")), P(("enc", "pool"), None))
    out_specs = P(("enc", "pool"), None)
    return jax.shard_map(shards, mesh=mesh, in_specs=in_specs, out_specs=out_specs, check_vma=False)
```

```python
import jax
import jax.numpy as jnp
from jax import lax
from jax.sharding import PartitionSpec as P


def lane_group_sum(x, group):
    n = x.shape[1]
    if 128 % group or n % 128:
        return x.reshape(x.shape[0], n // group, group).sum(axis=1)
    partial = x[:, :128]
    for k in range(1, n // 128):
        partial = partial + x[:, k * 128:(k + 1) * 128]
    total = partial[:, :group]
    for g in range(1, 128 // group):
        total = total + partial[:, g * group:(g + 1) * group]
    return total


def tile_scores(query, query_bias, other, other_bias):
    tok, query_items, width = query.shape
    other_items = other.shape[1]
    rows = min(32, query_items)
    blocks = query_items // rows
    other_flat = other.reshape(tok * other_items, width)
    other_add = other_bias.astype(jnp.float32)[:, :, None]
    other_valid = other_bias == 0
    turned_all = jnp.transpose(query.reshape(tok, blocks, rows, width), (1, 0, 2, 3))
    adding_all = jnp.transpose(query_bias.astype(jnp.float32).reshape(tok, blocks, rows), (1, 0, 2))[..., None]
    kept_all = jnp.transpose((query_bias == 0).reshape(tok, blocks, rows), (1, 0, 2))

    def one_block(operands):
        turned, adding, kept = operands
        flat = turned.reshape(tok * rows, width)
        dots_fore = jnp.einsum("ubh,qh->ubq", other, flat, preferred_element_type=jnp.float32)
        fore = jnp.max(dots_fore + other_add, axis=0)
        fore = lane_group_sum(jnp.where(kept.reshape(1, tok * rows), fore, 0.0), rows)
        dots_back = jnp.einsum("trh,ch->trc", turned, other_flat, preferred_element_type=jnp.float32)
        back = jnp.max(dots_back + adding, axis=0)
        back = lane_group_sum(jnp.where(other_valid.reshape(1, -1), back, 0.0), other_items)
        return 0.5 * (fore.T + back)

    result = lax.map(one_block, (turned_all, adding_all, kept_all))
    return result.reshape(query_items, other_items)


def shards(encoded, slot_items, lengths, token_mask):
    n_enc = lax.axis_size("enc")
    n_pool = lax.axis_size("pool")
    owners = n_enc * n_pool
    group = encoded.shape[0]
    toks = encoded.shape[1]
    width = encoded.shape[2]
    items_dev = lengths.shape[0]
    per = items_dev // n_pool
    tok = n_enc * toks
    n_tok = items_dev * tok
    pool_index = lax.axis_index("pool")

    table = slot_items.reshape(owners, n_pool, per)
    mine = lax.dynamic_index_in_dim(table, pool_index, 1, keepdims=False) - pool_index * group
    outgoing = jnp.take(encoded, mine, axis=0, mode="clip")
    outgoing = jnp.transpose(outgoing, (2, 0, 1, 3))
    arrived = lax.all_to_all(outgoing, ("enc", "pool"), split_axis=1, concat_axis=1, tiled=True)
    slotted = arrived.reshape(tok, items_dev, width)
    values = slotted.astype(jnp.float32)
    normed = (values / jnp.sqrt(jnp.sum(values * values, axis=-1, keepdims=True) + 1e-06)).astype(
        jnp.bfloat16
    )
    position = jnp.arange(tok, dtype=jnp.int32)[None, :]
    valid = (position < lengths[:, None]) & ((position == 0) | (token_mask == 1))
    valid_tm = jnp.transpose(valid.reshape(items_dev, n_enc, toks), (2, 1, 0)).reshape(tok, items_dev)
    bias = jnp.where(valid_tm, 0.0, -4.0).astype(jnp.bfloat16)
    packed = jnp.concatenate([normed.reshape(n_tok, width), bias.reshape(-1, width)], axis=0)
    block = packed[:n_tok].reshape(tok, items_dev, width)

    parity = (pool_index ^ (pool_index >> 1) ^ (pool_index >> 2)) & 1
    is_a = (pool_index & 1) == 0

    def par(p):
        return (p ^ (p >> 1) ^ (p >> 2)) & 1

    send_pairs = [(p, p ^ (4 if par(p) else 2)) for p in range(n_pool)]
    back_pairs = [(t, s) for s, t in send_pairs]
    chip_pairs = [(p, p ^ 1) for p in range(n_pool)]

    z_recv = lax.ppermute(packed, "pool", send_pairs)
    c_recv = lax.ppermute(packed, "pool", chip_pairs)

    def unpack(received):
        return received[:n_tok].reshape(tok, items_dev, width), received[n_tok:].reshape(tok, items_dev)

    half = items_dev // 2
    c_blk, c_bias = unpack(c_recv)
    query = jnp.where(is_a, block[:, :half], c_blk[:, half:])
    query_bias = jnp.where(is_a, bias[:, :half], c_bias[:, half:])
    other = jnp.where(is_a, c_blk, block)
    other_bias = jnp.where(is_a, c_bias, bias)
    part = tile_scores(query, query_bias, other, other_bias)
    part_recv = lax.ppermute(part, "pool", chip_pairs)
    joined = jnp.where(
        is_a,
        jnp.concatenate([part, part_recv], axis=0),
        jnp.concatenate([part_recv, part], axis=0),
    )
    tile0 = jnp.where(is_a, joined, joined.T)

    z_blk, z_bias = unpack(z_recv)
    tile_z = tile_scores(block, bias, z_blk, z_bias)
    tile_back = lax.ppermute(tile_z.T, "pool", back_pairs)
    via_bit1 = parity == 1
    col1 = jnp.where(via_bit1, tile_z, tile_back)
    col2 = jnp.where(via_bit1, tile_back, tile_z)
    return jnp.concatenate([tile0, col1, col2], axis=1)


def solution(mesh):
    in_specs = (P("pool", "enc", None), P(), P(("enc", "pool")), P(("enc", "pool"), None))
    out_specs = P(("enc", "pool"), None)
    return jax.shard_map(shards, mesh=mesh, in_specs=in_specs, out_specs=out_specs, check_vma=False)
```

```python
import jax
import jax.numpy as jnp
from jax import lax
from jax.sharding import PartitionSpec as P


def tile_scores(query, query_bias, other, other_bias):
    tok, query_items, width = query.shape
    other_items = other.shape[1]
    rows = min(32, query_items)
    blocks = query_items // rows
    other_flat = other.reshape(tok * other_items, width)
    other_add = other_bias.astype(jnp.float32)[:, :, None]
    other_valid = other_bias == 0
    turned_all = jnp.transpose(query.reshape(tok, blocks, rows, width), (1, 0, 2, 3))
    adding_all = jnp.transpose(query_bias.astype(jnp.float32).reshape(tok, blocks, rows), (1, 0, 2))[..., None]
    kept_all = jnp.transpose((query_bias == 0).reshape(tok, blocks, rows), (1, 0, 2))

    def one_block(operands):
        turned, adding, kept = operands
        flat = turned.reshape(tok * rows, width)
        dots_fore = jnp.einsum("ubh,qh->ubq", other, flat, preferred_element_type=jnp.float32)
        fore = jnp.max(dots_fore + other_add, axis=0).reshape(other_items, tok, rows)
        fore = jnp.sum(jnp.where(kept[None], fore, 0.0), axis=1)
        dots_back = jnp.einsum("trh,ch->trc", turned, other_flat, preferred_element_type=jnp.float32)
        back = jnp.max(dots_back + adding, axis=0).reshape(rows, tok, other_items)
        back = jnp.sum(jnp.where(other_valid[None], back, 0.0), axis=1)
        return 0.5 * (fore.T + back)

    result = lax.map(one_block, (turned_all, adding_all, kept_all))
    return result.reshape(query_items, other_items)


def shards(encoded, slot_items, lengths, token_mask):
    n_enc = lax.axis_size("enc")
    n_pool = lax.axis_size("pool")
    owners = n_enc * n_pool
    group = encoded.shape[0]
    toks = encoded.shape[1]
    width = encoded.shape[2]
    items_dev = lengths.shape[0]
    per = items_dev // n_pool
    tok = n_enc * toks
    n_tok = items_dev * tok
    pool_index = lax.axis_index("pool")

    table = slot_items.reshape(owners, n_pool, per)
    mine = lax.dynamic_index_in_dim(table, pool_index, 1, keepdims=False) - pool_index * group
    outgoing = jnp.take(encoded, mine, axis=0, mode="clip")
    outgoing = jnp.transpose(outgoing, (2, 0, 1, 3))
    arrived = lax.all_to_all(outgoing, ("enc", "pool"), split_axis=1, concat_axis=1, tiled=True)
    slotted = arrived.reshape(tok, items_dev, width)
    values = slotted.astype(jnp.float32)
    normed = (values / jnp.sqrt(jnp.sum(values * values, axis=-1, keepdims=True) + 1e-06)).astype(
        jnp.bfloat16
    )
    position = jnp.arange(tok, dtype=jnp.int32)[None, :]
    valid = (position < lengths[:, None]) & ((position == 0) | (token_mask == 1))
    valid_tm = jnp.transpose(valid.reshape(items_dev, n_enc, toks), (2, 1, 0)).reshape(tok, items_dev)
    bias = jnp.where(valid_tm, 0.0, -4.0).astype(jnp.bfloat16)
    packed = jnp.concatenate([normed.reshape(n_tok, width), bias.reshape(-1, width)], axis=0)
    block = packed[:n_tok].reshape(tok, items_dev, width)

    parity = (pool_index ^ (pool_index >> 1) ^ (pool_index >> 2)) & 1
    is_a = (pool_index & 1) == 0

    def par(p):
        return (p ^ (p >> 1) ^ (p >> 2)) & 1

    send_pairs = [(p, p ^ (4 if par(p) else 2)) for p in range(n_pool)]
    back_pairs = [(t, s) for s, t in send_pairs]
    chip_pairs = [(p, p ^ 1) for p in range(n_pool)]

    z_recv = lax.ppermute(packed, "pool", send_pairs)
    c_recv = lax.ppermute(packed, "pool", chip_pairs)

    def unpack(received):
        return received[:n_tok].reshape(tok, items_dev, width), received[n_tok:].reshape(tok, items_dev)

    half = items_dev // 2
    c_blk, c_bias = unpack(c_recv)
    query = jnp.where(is_a, block[:, :half], c_blk[:, half:])
    query_bias = jnp.where(is_a, bias[:, :half], c_bias[:, half:])
    other = jnp.where(is_a, c_blk, block)
    other_bias = jnp.where(is_a, c_bias, bias)
    part = tile_scores(query, query_bias, other, other_bias)
    part_recv = lax.ppermute(part, "pool", chip_pairs)
    joined = jnp.where(
        is_a,
        jnp.concatenate([part, part_recv], axis=0),
        jnp.concatenate([part_recv, part], axis=0),
    )
    tile0 = jnp.where(is_a, joined, joined.T)

    z_blk, z_bias = unpack(z_recv)
    tile_z = tile_scores(block, bias, z_blk, z_bias)
    tile_back = lax.ppermute(tile_z.T, "pool", back_pairs)
    other_items = tile_z.shape[1]
    ready = lax.optimization_barrier(jnp.concatenate([tile0, tile_z, tile_z], axis=1))
    column = jnp.arange(3 * other_items, dtype=jnp.int32)[None, :] // other_items
    back_here = column == 1 + parity
    return jnp.where(back_here, jnp.tile(tile_back, (1, 3)), ready)


def solution(mesh):
    in_specs = (P("pool", "enc", None), P(), P(("enc", "pool")), P(("enc", "pool"), None))
    out_specs = P(("enc", "pool"), None)
    return jax.shard_map(shards, mesh=mesh, in_specs=in_specs, out_specs=out_specs, check_vma=False)
```

```python
import functools

import jax
import jax.numpy as jnp
from jax import lax
from jax.experimental import pallas as pl
from jax.experimental.pallas import tpu as pltpu
from jax.sharding import PartitionSpec as P


def tile_scores(query, query_bias, other, other_bias):
    tok, query_items, width = query.shape
    other_items = other.shape[1]
    rows = min(32, query_items)
    blocks = query_items // rows
    other_flat = other.reshape(tok * other_items, width)
    other_add = other_bias.astype(jnp.float32)[:, :, None]
    other_valid = other_bias == 0
    turned_all = jnp.transpose(query.reshape(tok, blocks, rows, width), (1, 0, 2, 3))
    adding_all = jnp.transpose(query_bias.astype(jnp.float32).reshape(tok, blocks, rows), (1, 0, 2))[..., None]
    kept_all = jnp.transpose((query_bias == 0).reshape(tok, blocks, rows), (1, 0, 2))

    def one_block(operands):
        turned, adding, kept = operands
        flat = turned.reshape(tok * rows, width)
        dots_fore = jnp.einsum("ubh,qh->ubq", other, flat, preferred_element_type=jnp.float32)
        fore = jnp.max(dots_fore + other_add, axis=0).reshape(other_items, tok, rows)
        fore = jnp.sum(jnp.where(kept[None], fore, 0.0), axis=1)
        dots_back = jnp.einsum("trh,ch->trc", turned, other_flat, preferred_element_type=jnp.float32)
        back = jnp.max(dots_back + adding, axis=0).reshape(rows, tok, other_items)
        back = jnp.sum(jnp.where(other_valid[None], back, 0.0), axis=1)
        return 0.5 * (fore.T + back)

    result = lax.map(one_block, (turned_all, adding_all, kept_all))
    return result.reshape(query_items, other_items)


def _chamfer_kernel(tok, nq, no, cw, q_ref, o_ref, qv_ref, ov_ref, out_ref, fm_ref):
    q = q_ref[...]
    acc_b = jnp.zeros((nq, 128), jnp.float32)
    for c in range(tok * no // cw):
        o_c = o_ref[c * cw:(c + 1) * cw, :]
        d = lax.dot_general(q, o_c, (((1,), (1,)), ((), ())), preferred_element_type=jnp.float32)
        m = d[:, 0:128]
        for k in range(1, cw // 128):
            m = jnp.maximum(m, d[:, k * 128:(k + 1) * 128])
        if c == 0:
            fm_ref[...] = m
        else:
            fm_ref[...] = jnp.maximum(fm_ref[...], m)
        mb = jnp.max(d.reshape(tok, nq, cw), axis=0)
        mbm = jnp.where(ov_ref[:, c * cw:(c + 1) * cw] > 0, mb, 0.0)
        s = mbm[:, 0:128]
        for k in range(1, cw // 128):
            s = s + mbm[:, k * 128:(k + 1) * 128]
        acc_b = acc_b + s
    fm = fm_ref[...]
    fm = jnp.maximum(fm, pltpu.roll(fm, 64, 1))
    fsum = jnp.sum(jnp.where(qv_ref[...] > 0, fm, 0.0).reshape(tok, nq, 128), axis=0)
    bsum = acc_b + pltpu.roll(acc_b, 64, 1)
    out_ref[...] = (0.5 * (fsum + bsum))[:, :no]


def chamfer_tile(query, query_valid, other, other_valid):
    tok, nq, width = query.shape
    no = other.shape[1]
    if no != 64 or (tok * no) % 512 or nq % 8:
        return tile_scores(
            query, jnp.where(query_valid, 0.0, -4.0), other, jnp.where(other_valid, 0.0, -4.0)
        )
    tok_nq, tok_no, cw = tok * nq, tok * no, 512
    q = query.reshape(tok_nq, width)
    o = other.reshape(tok_no, width)
    qv = jnp.broadcast_to(query_valid.astype(jnp.float32).reshape(tok_nq, 1), (tok_nq, 128))
    ov = other_valid.astype(jnp.float32).reshape(1, tok_no)
    kernel = functools.partial(_chamfer_kernel, tok, nq, no, cw)
    return pl.pallas_call(
        kernel,
        out_shape=jax.ShapeDtypeStruct((nq, no), jnp.float32),
        in_specs=[pl.BlockSpec(memory_space=pltpu.VMEM)] * 4,
        out_specs=pl.BlockSpec(memory_space=pltpu.VMEM),
        scratch_shapes=[pltpu.VMEM((tok_nq, 128), jnp.float32)],
        cost_estimate=pl.CostEstimate(
            flops=2 * tok_nq * tok_no * width, transcendentals=0, bytes_accessed=(tok_nq + tok_no) * width * 2
        ),
    )(q, o, qv, ov)


def shards(encoded, slot_items, lengths, token_mask):
    n_enc = lax.axis_size("enc")
    n_pool = lax.axis_size("pool")
    owners = n_enc * n_pool
    group = encoded.shape[0]
    toks = encoded.shape[1]
    width = encoded.shape[2]
    items_dev = lengths.shape[0]
    per = items_dev // n_pool
    tok = n_enc * toks
    n_tok = items_dev * tok
    pool_index = lax.axis_index("pool")

    table = slot_items.reshape(owners, n_pool, per)
    mine = lax.dynamic_index_in_dim(table, pool_index, 1, keepdims=False) - pool_index * group
    outgoing = jnp.take(encoded, mine, axis=0, mode="clip")
    outgoing = jnp.transpose(outgoing, (2, 0, 1, 3))
    arrived = lax.all_to_all(outgoing, ("enc", "pool"), split_axis=1, concat_axis=1, tiled=True)
    slotted = arrived.reshape(tok, items_dev, width)
    values = slotted.astype(jnp.float32)
    normed = (values / jnp.sqrt(jnp.sum(values * values, axis=-1, keepdims=True) + 1e-06)).astype(
        jnp.bfloat16
    )
    position = jnp.arange(tok, dtype=jnp.int32)[None, :]
    valid = (position < lengths[:, None]) & ((position == 0) | (token_mask == 1))
    valid_tm = jnp.transpose(valid.reshape(items_dev, n_enc, toks), (2, 1, 0)).reshape(tok, items_dev)
    bias = jnp.where(valid_tm, 0.0, -4.0).astype(jnp.bfloat16)
    normed = jnp.where(valid_tm[:, :, None], normed, normed[0][None])
    packed = jnp.concatenate([normed.reshape(n_tok, width), bias.reshape(-1, width)], axis=0)
    block = packed[:n_tok].reshape(tok, items_dev, width)

    parity = (pool_index ^ (pool_index >> 1) ^ (pool_index >> 2)) & 1
    is_a = (pool_index & 1) == 0

    def par(p):
        return (p ^ (p >> 1) ^ (p >> 2)) & 1

    send_pairs = [(p, p ^ (4 if par(p) else 2)) for p in range(n_pool)]
    back_pairs = [(t, s) for s, t in send_pairs]
    chip_pairs = [(p, p ^ 1) for p in range(n_pool)]

    z_recv = lax.ppermute(packed, "pool", send_pairs)
    c_recv = lax.ppermute(packed, "pool", chip_pairs)

    def unpack(received):
        return received[:n_tok].reshape(tok, items_dev, width), received[n_tok:].reshape(tok, items_dev)

    half = items_dev // 2
    c_blk, c_bias = unpack(c_recv)
    query = jnp.where(is_a, block[:, :half], c_blk[:, half:])
    query_bias = jnp.where(is_a, bias[:, :half], c_bias[:, half:])
    other = jnp.where(is_a, c_blk, block)
    other_bias = jnp.where(is_a, c_bias, bias)
    part = chamfer_tile(query, query_bias == 0, other, other_bias == 0)
    part_recv = lax.ppermute(part, "pool", chip_pairs)
    joined = jnp.where(
        is_a,
        jnp.concatenate([part, part_recv], axis=0),
        jnp.concatenate([part_recv, part], axis=0),
    )
    tile0 = jnp.where(is_a, joined, joined.T)

    z_blk, z_bias = unpack(z_recv)
    tile_z = chamfer_tile(block, valid_tm, z_blk, z_bias == 0)
    tile_back = lax.ppermute(tile_z.T, "pool", back_pairs)
    via_bit1 = parity == 1
    col1 = jnp.where(via_bit1, tile_z, tile_back)
    col2 = jnp.where(via_bit1, tile_back, tile_z)
    return jnp.concatenate([tile0, col1, col2], axis=1)


def solution(mesh):
    in_specs = (P("pool", "enc", None), P(), P(("enc", "pool")), P(("enc", "pool"), None))
    out_specs = P(("enc", "pool"), None)
    return jax.shard_map(shards, mesh=mesh, in_specs=in_specs, out_specs=out_specs, check_vma=False)
```

```python
import functools

import jax
import jax.numpy as jnp
from jax import lax
from jax.experimental import pallas as pl
from jax.experimental.pallas import tpu as pltpu
from jax.sharding import PartitionSpec as P


def tile_scores(query, query_bias, other, other_bias):
    tok, query_items, width = query.shape
    other_items = other.shape[1]
    rows = min(32, query_items)
    blocks = query_items // rows
    other_flat = other.reshape(tok * other_items, width)
    other_add = other_bias.astype(jnp.float32)[:, :, None]
    other_valid = other_bias == 0
    turned_all = jnp.transpose(query.reshape(tok, blocks, rows, width), (1, 0, 2, 3))
    adding_all = jnp.transpose(query_bias.astype(jnp.float32).reshape(tok, blocks, rows), (1, 0, 2))[..., None]
    kept_all = jnp.transpose((query_bias == 0).reshape(tok, blocks, rows), (1, 0, 2))

    def one_block(operands):
        turned, adding, kept = operands
        flat = turned.reshape(tok * rows, width)
        dots_fore = jnp.einsum("ubh,qh->ubq", other, flat, preferred_element_type=jnp.float32)
        fore = jnp.max(dots_fore + other_add, axis=0).reshape(other_items, tok, rows)
        fore = jnp.sum(jnp.where(kept[None], fore, 0.0), axis=1)
        dots_back = jnp.einsum("trh,ch->trc", turned, other_flat, preferred_element_type=jnp.float32)
        back = jnp.max(dots_back + adding, axis=0).reshape(rows, tok, other_items)
        back = jnp.sum(jnp.where(other_valid[None], back, 0.0), axis=1)
        return 0.5 * (fore.T + back)

    result = lax.map(one_block, (turned_all, adding_all, kept_all))
    return result.reshape(query_items, other_items)


def _chamfer_kernel(tok, nq, no, cw, q_ref, o_ref, qv_ref, out_ref, out_t_ref, fm_ref):
    q = q_ref[...]
    n_rows = tok * no // 128
    flags = o_ref[tok * no:tok * no + n_rows, :].astype(jnp.float32)
    acc_b = jnp.zeros((nq, 128), jnp.float32)
    for c in range(tok * no // cw):
        o_c = o_ref[c * cw:(c + 1) * cw, :]
        d = lax.dot_general(q, o_c, (((1,), (1,)), ((), ())), preferred_element_type=jnp.float32)
        m = d[:, 0:128]
        for k in range(1, cw // 128):
            m = jnp.maximum(m, d[:, k * 128:(k + 1) * 128])
        if c == 0:
            fm_ref[...] = m
        else:
            fm_ref[...] = jnp.maximum(fm_ref[...], m)
        mb = jnp.max(d.reshape(tok, nq, cw), axis=0)
        for k in range(cw // 128):
            row = c * (cw // 128) + k
            acc_b = acc_b + jnp.where(flags[row:row + 1, :] == 0, mb[:, k * 128:(k + 1) * 128], 0.0)
    fm = fm_ref[...]
    fm = jnp.maximum(fm, pltpu.roll(fm, 64, 1))
    fsum = jnp.sum(jnp.where(qv_ref[...] > 0, fm, 0.0).reshape(tok, nq, 128), axis=0)
    bsum = acc_b + pltpu.roll(acc_b, 64, 1)
    res = 0.5 * (fsum + bsum)
    out_ref[...] = res[:, :no]
    out_t_ref[...] = res.T[:no, :]


def chamfer_tile(query, query_valid, other_packed, tok):
    tok_nq, width = query.shape
    nq = tok_nq // tok
    no = 64
    cw = 512
    kernel = functools.partial(_chamfer_kernel, tok, nq, no, cw)
    return pl.pallas_call(
        kernel,
        out_shape=(jax.ShapeDtypeStruct((nq, no), jnp.float32), jax.ShapeDtypeStruct((no, nq), jnp.float32)),
        in_specs=[pl.BlockSpec(memory_space=pltpu.VMEM)] * 3,
        out_specs=(pl.BlockSpec(memory_space=pltpu.VMEM), pl.BlockSpec(memory_space=pltpu.VMEM)),
        scratch_shapes=[pltpu.VMEM((tok_nq, 128), jnp.float32)],
        cost_estimate=pl.CostEstimate(
            flops=2 * tok_nq * tok * no * width, transcendentals=0, bytes_accessed=(tok_nq + tok * no) * width * 2
        ),
    )(query, other_packed, query_valid)


def shards(encoded, slot_items, lengths, token_mask):
    n_enc = lax.axis_size("enc")
    n_pool = lax.axis_size("pool")
    owners = n_enc * n_pool
    group = encoded.shape[0]
    toks = encoded.shape[1]
    width = encoded.shape[2]
    items_dev = lengths.shape[0]
    per = items_dev // n_pool
    tok = n_enc * toks
    n_tok = items_dev * tok
    pool_index = lax.axis_index("pool")

    table = slot_items.reshape(owners, n_pool, per)
    mine = lax.dynamic_index_in_dim(table, pool_index, 1, keepdims=False) - pool_index * group
    outgoing = jnp.take(encoded, mine, axis=0, mode="clip")
    outgoing = jnp.transpose(outgoing, (2, 0, 1, 3))
    arrived = lax.all_to_all(outgoing, ("enc", "pool"), split_axis=1, concat_axis=1, tiled=True)
    slotted = arrived.reshape(tok, items_dev, width)
    values = slotted.astype(jnp.float32)
    normed = (values / jnp.sqrt(jnp.sum(values * values, axis=-1, keepdims=True) + 1e-06)).astype(
        jnp.bfloat16
    )
    position = jnp.arange(tok, dtype=jnp.int32)[None, :]
    valid = (position < lengths[:, None]) & ((position == 0) | (token_mask == 1))
    valid_tm = jnp.transpose(valid.reshape(items_dev, n_enc, toks), (2, 1, 0)).reshape(tok, items_dev)
    bias = jnp.where(valid_tm, 0.0, -4.0).astype(jnp.bfloat16)
    normed = jnp.where(valid_tm[:, :, None], normed, normed[0][None])
    packed = jnp.concatenate([normed.reshape(n_tok, width), bias.reshape(-1, width)], axis=0)
    block = packed[:n_tok].reshape(tok, items_dev, width)

    parity = (pool_index ^ (pool_index >> 1) ^ (pool_index >> 2)) & 1
    is_a = (pool_index & 1) == 0

    def par(p):
        return (p ^ (p >> 1) ^ (p >> 2)) & 1

    send_pairs = [(p, p ^ (4 if par(p) else 2)) for p in range(n_pool)]
    back_pairs = [(t, s) for s, t in send_pairs]
    chip_pairs = [(p, p ^ 1) for p in range(n_pool)]

    z_recv = lax.ppermute(packed, "pool", send_pairs)
    c_recv = lax.ppermute(packed, "pool", chip_pairs)

    def row_flags(valid_rows):
        return jnp.broadcast_to(valid_rows.astype(jnp.float32).reshape(-1, 1), (valid_rows.size, 128))

    half = items_dev // 2
    own_flags = row_flags(valid_tm)
    c_blk = c_recv[:n_tok].reshape(tok, items_dev, width)
    c_valid = c_recv[n_tok:].reshape(tok, items_dev) == 0
    query = jnp.where(is_a, block[:, :half], c_blk[:, half:]).reshape(tok * half, width)
    query_flags = row_flags(jnp.where(is_a, valid_tm[:, :half], c_valid[:, half:]))
    other_packed = jnp.where(is_a, c_recv, packed)
    part, _ = chamfer_tile(query, query_flags, other_packed, tok)
    part, own_flags = lax.optimization_barrier((part, own_flags))
    part_recv = lax.ppermute(part, "pool", chip_pairs)
    joined = jnp.where(
        is_a,
        jnp.concatenate([part, part_recv], axis=0),
        jnp.concatenate([part_recv, part], axis=0),
    )
    tile0 = jnp.where(is_a, joined, joined.T)

    tile_z, tile_z_t = chamfer_tile(block.reshape(n_tok, width), own_flags, z_recv, tok)
    tile_back = lax.ppermute(tile_z_t, "pool", back_pairs)
    via_bit1 = parity == 1
    col1 = jnp.where(via_bit1, tile_z, tile_back)
    col2 = jnp.where(via_bit1, tile_back, tile_z)
    return jnp.concatenate([tile0, col1, col2], axis=1)


def solution(mesh):
    in_specs = (P("pool", "enc", None), P(), P(("enc", "pool")), P(("enc", "pool"), None))
    out_specs = P(("enc", "pool"), None)
    return jax.shard_map(shards, mesh=mesh, in_specs=in_specs, out_specs=out_specs, check_vma=False)
```

```python
import functools

import jax
import jax.numpy as jnp
from jax import lax
from jax.experimental import pallas as pl
from jax.experimental.pallas import tpu as pltpu
from jax.sharding import PartitionSpec as P


def tile_scores(query, query_bias, other, other_bias):
    tok, query_items, width = query.shape
    other_items = other.shape[1]
    rows = min(32, query_items)
    blocks = query_items // rows
    other_flat = other.reshape(tok * other_items, width)
    other_add = other_bias.astype(jnp.float32)[:, :, None]
    other_valid = other_bias == 0
    turned_all = jnp.transpose(query.reshape(tok, blocks, rows, width), (1, 0, 2, 3))
    adding_all = jnp.transpose(query_bias.astype(jnp.float32).reshape(tok, blocks, rows), (1, 0, 2))[..., None]
    kept_all = jnp.transpose((query_bias == 0).reshape(tok, blocks, rows), (1, 0, 2))

    def one_block(operands):
        turned, adding, kept = operands
        flat = turned.reshape(tok * rows, width)
        dots_fore = jnp.einsum("ubh,qh->ubq", other, flat, preferred_element_type=jnp.float32)
        fore = jnp.max(dots_fore + other_add, axis=0).reshape(other_items, tok, rows)
        fore = jnp.sum(jnp.where(kept[None], fore, 0.0), axis=1)
        dots_back = jnp.einsum("trh,ch->trc", turned, other_flat, preferred_element_type=jnp.float32)
        back = jnp.max(dots_back + adding, axis=0).reshape(rows, tok, other_items)
        back = jnp.sum(jnp.where(other_valid[None], back, 0.0), axis=1)
        return 0.5 * (fore.T + back)

    result = lax.map(one_block, (turned_all, adding_all, kept_all))
    return result.reshape(query_items, other_items)


def _chamfer_kernel(tok, nq, no, cw, q_ref, o_hbm, qv_ref, out_ref, out_t_ref, fm_ref, o_buf, f_buf, sems):
    n_chunks = tok * no // cw
    n_rows = tok * no // 128

    def chunk_copy(c):
        return pltpu.make_async_copy(o_hbm.at[pl.ds(c * cw, cw), :], o_buf.at[c % 2], sems.at[c % 2])

    flag_copy = pltpu.make_async_copy(o_hbm.at[pl.ds(tok * no, n_rows), :], f_buf, sems.at[2])
    flag_copy.start()
    chunk_copy(0).start()
    q = q_ref[...]
    flag_copy.wait()
    flags = f_buf[...].astype(jnp.float32)
    acc_b = jnp.zeros((nq, 128), jnp.float32)
    for c in range(n_chunks):
        if c + 1 < n_chunks:
            chunk_copy(c + 1).start()
        chunk_copy(c).wait()
        o_c = o_buf[c % 2]
        d = lax.dot_general(q, o_c, (((1,), (1,)), ((), ())), preferred_element_type=jnp.float32)
        m = d[:, 0:128]
        for k in range(1, cw // 128):
            m = jnp.maximum(m, d[:, k * 128:(k + 1) * 128])
        if c == 0:
            fm_ref[...] = m
        else:
            fm_ref[...] = jnp.maximum(fm_ref[...], m)
        mb = jnp.max(d.reshape(tok, nq, cw), axis=0)
        for k in range(cw // 128):
            row = c * (cw // 128) + k
            acc_b = acc_b + jnp.where(flags[row:row + 1, :] == 0, mb[:, k * 128:(k + 1) * 128], 0.0)
    fm = fm_ref[...]
    fm = jnp.maximum(fm, pltpu.roll(fm, 64, 1))
    fsum = jnp.sum(jnp.where(qv_ref[...] > 0, fm, 0.0).reshape(tok, nq, 128), axis=0)
    bsum = acc_b + pltpu.roll(acc_b, 64, 1)
    res = 0.5 * (fsum + bsum)
    out_ref[...] = res[:, :no]
    out_t_ref[...] = res.T[:no, :]


def chamfer_tile(query, query_valid, other_packed, tok):
    tok_nq, width = query.shape
    nq = tok_nq // tok
    no = 64
    cw = 512
    kernel = functools.partial(_chamfer_kernel, tok, nq, no, cw)
    return pl.pallas_call(
        kernel,
        out_shape=(jax.ShapeDtypeStruct((nq, no), jnp.float32), jax.ShapeDtypeStruct((no, nq), jnp.float32)),
        in_specs=[
            pl.BlockSpec(memory_space=pltpu.VMEM),
            pl.BlockSpec(memory_space=pl.ANY),
            pl.BlockSpec(memory_space=pltpu.VMEM),
        ],
        out_specs=(pl.BlockSpec(memory_space=pltpu.VMEM), pl.BlockSpec(memory_space=pltpu.VMEM)),
        scratch_shapes=[
            pltpu.VMEM((tok_nq, 128), jnp.float32),
            pltpu.VMEM((2, cw, width), jnp.bfloat16),
            pltpu.VMEM((tok * no // 128, width), jnp.bfloat16),
            pltpu.SemaphoreType.DMA((3,)),
        ],
        cost_estimate=pl.CostEstimate(
            flops=2 * tok_nq * tok * no * width, transcendentals=0, bytes_accessed=(tok_nq + tok * no) * width * 2
        ),
    )(query, other_packed, query_valid)


def shards(encoded, slot_items, lengths, token_mask):
    n_enc = lax.axis_size("enc")
    n_pool = lax.axis_size("pool")
    owners = n_enc * n_pool
    group = encoded.shape[0]
    toks = encoded.shape[1]
    width = encoded.shape[2]
    items_dev = lengths.shape[0]
    per = items_dev // n_pool
    tok = n_enc * toks
    n_tok = items_dev * tok
    pool_index = lax.axis_index("pool")

    table = slot_items.reshape(owners, n_pool, per)
    mine = lax.dynamic_index_in_dim(table, pool_index, 1, keepdims=False) - pool_index * group
    outgoing = jnp.take(encoded, mine, axis=0, mode="clip")
    outgoing = jnp.transpose(outgoing, (2, 0, 1, 3))
    arrived = lax.all_to_all(outgoing, ("enc", "pool"), split_axis=1, concat_axis=1, tiled=True)
    slotted = arrived.reshape(tok, items_dev, width)
    values = slotted.astype(jnp.float32)
    normed = (values / jnp.sqrt(jnp.sum(values * values, axis=-1, keepdims=True) + 1e-06)).astype(
        jnp.bfloat16
    )
    position = jnp.arange(tok, dtype=jnp.int32)[None, :]
    valid = (position < lengths[:, None]) & ((position == 0) | (token_mask == 1))
    valid_tm = jnp.transpose(valid.reshape(items_dev, n_enc, toks), (2, 1, 0)).reshape(tok, items_dev)
    bias = jnp.where(valid_tm, 0.0, -4.0).astype(jnp.bfloat16)
    normed = jnp.where(valid_tm[:, :, None], normed, normed[0][None])
    packed = jnp.concatenate([normed.reshape(n_tok, width), bias.reshape(-1, width)], axis=0)
    block = packed[:n_tok].reshape(tok, items_dev, width)

    parity = (pool_index ^ (pool_index >> 1) ^ (pool_index >> 2)) & 1
    is_a = (pool_index & 1) == 0

    def par(p):
        return (p ^ (p >> 1) ^ (p >> 2)) & 1

    send_pairs = [(p, p ^ (4 if par(p) else 2)) for p in range(n_pool)]
    back_pairs = [(t, s) for s, t in send_pairs]
    chip_pairs = [(p, p ^ 1) for p in range(n_pool)]

    z_recv = lax.ppermute(packed, "pool", send_pairs)
    c_recv = lax.ppermute(packed, "pool", chip_pairs)

    def row_flags(valid_rows):
        return jnp.broadcast_to(valid_rows.astype(jnp.float32).reshape(-1, 1), (valid_rows.size, 128))

    half = items_dev // 2
    own_flags = row_flags(valid_tm)
    c_blk = c_recv[:n_tok].reshape(tok, items_dev, width)
    c_valid = c_recv[n_tok:].reshape(tok, items_dev) == 0
    query = jnp.where(is_a, block[:, :half], c_blk[:, half:]).reshape(tok * half, width)
    query_flags = row_flags(jnp.where(is_a, valid_tm[:, :half], c_valid[:, half:]))
    other_packed = jnp.where(is_a, c_recv, packed)
    part, _ = chamfer_tile(query, query_flags, other_packed, tok)
    part, own_flags = lax.optimization_barrier((part, own_flags))
    part_recv = lax.ppermute(part, "pool", chip_pairs)
    joined = jnp.where(
        is_a,
        jnp.concatenate([part, part_recv], axis=0),
        jnp.concatenate([part_recv, part], axis=0),
    )
    tile0 = jnp.where(is_a, joined, joined.T)
    tile0, z_recv = lax.optimization_barrier((tile0, z_recv))

    tile_z, tile_z_t = chamfer_tile(block.reshape(n_tok, width), own_flags, z_recv, tok)
    tile_back = lax.ppermute(tile_z_t, "pool", back_pairs)
    via_bit1 = parity == 1
    col1 = jnp.where(via_bit1, tile_z, tile_back)
    col2 = jnp.where(via_bit1, tile_back, tile_z)
    return jnp.concatenate([tile0, col1, col2], axis=1)


def solution(mesh):
    in_specs = (P("pool", "enc", None), P(), P(("enc", "pool")), P(("enc", "pool"), None))
    out_specs = P(("enc", "pool"), None)
    return jax.shard_map(shards, mesh=mesh, in_specs=in_specs, out_specs=out_specs, check_vma=False)
```

```python
import functools

import jax
import jax.numpy as jnp
from jax import lax
from jax.experimental import pallas as pl
from jax.experimental.pallas import tpu as pltpu
from jax.sharding import PartitionSpec as P


def tile_scores(query, query_bias, other, other_bias):
    tok, query_items, width = query.shape
    other_items = other.shape[1]
    rows = min(32, query_items)
    blocks = query_items // rows
    other_flat = other.reshape(tok * other_items, width)
    other_add = other_bias.astype(jnp.float32)[:, :, None]
    other_valid = other_bias == 0
    turned_all = jnp.transpose(query.reshape(tok, blocks, rows, width), (1, 0, 2, 3))
    adding_all = jnp.transpose(query_bias.astype(jnp.float32).reshape(tok, blocks, rows), (1, 0, 2))[..., None]
    kept_all = jnp.transpose((query_bias == 0).reshape(tok, blocks, rows), (1, 0, 2))

    def one_block(operands):
        turned, adding, kept = operands
        flat = turned.reshape(tok * rows, width)
        dots_fore = jnp.einsum("ubh,qh->ubq", other, flat, preferred_element_type=jnp.float32)
        fore = jnp.max(dots_fore + other_add, axis=0).reshape(other_items, tok, rows)
        fore = jnp.sum(jnp.where(kept[None], fore, 0.0), axis=1)
        dots_back = jnp.einsum("trh,ch->trc", turned, other_flat, preferred_element_type=jnp.float32)
        back = jnp.max(dots_back + adding, axis=0).reshape(rows, tok, other_items)
        back = jnp.sum(jnp.where(other_valid[None], back, 0.0), axis=1)
        return 0.5 * (fore.T + back)

    result = lax.map(one_block, (turned_all, adding_all, kept_all))
    return result.reshape(query_items, other_items)


def _chamfer_kernel(tok, nq, no, cw, q_ref, o_ref, qv_ref, out_ref, out_t_ref, fm_ref):
    q = q_ref[...]
    n_rows = tok * no // 128
    flags = o_ref[tok * no:tok * no + n_rows, :].astype(jnp.float32)
    acc_b = jnp.zeros((nq, 128), jnp.float32)
    for c in range(tok * no // cw):
        o_c = o_ref[c * cw:(c + 1) * cw, :]
        d = lax.dot_general(q, o_c, (((1,), (1,)), ((), ())), preferred_element_type=jnp.float32)
        m = d[:, 0:128]
        for k in range(1, cw // 128):
            m = jnp.maximum(m, d[:, k * 128:(k + 1) * 128])
        if c == 0:
            fm_ref[...] = m
        else:
            fm_ref[...] = jnp.maximum(fm_ref[...], m)
        mb = jnp.max(d.reshape(tok, nq, cw), axis=0)
        for k in range(cw // 128):
            row = c * (cw // 128) + k
            acc_b = acc_b + jnp.where(flags[row:row + 1, :] == 0, mb[:, k * 128:(k + 1) * 128], 0.0)
    fm = fm_ref[...]
    fm = jnp.maximum(fm, pltpu.roll(fm, 64, 1))
    fsum = jnp.sum(jnp.where(qv_ref[...] > 0, fm, 0.0).reshape(tok, nq, 128), axis=0)
    bsum = acc_b + pltpu.roll(acc_b, 64, 1)
    res = 0.5 * (fsum + bsum)
    out_ref[...] = res[:, :no]
    out_t_ref[...] = res.T[:no, :]


def chamfer_tile(query, query_valid, other_packed, tok):
    tok_nq, width = query.shape
    nq = tok_nq // tok
    no = 64
    cw = 512
    kernel = functools.partial(_chamfer_kernel, tok, nq, no, cw)
    return pl.pallas_call(
        kernel,
        out_shape=(jax.ShapeDtypeStruct((nq, no), jnp.float32), jax.ShapeDtypeStruct((no, nq), jnp.float32)),
        in_specs=[pl.BlockSpec(memory_space=pltpu.VMEM)] * 3,
        out_specs=(pl.BlockSpec(memory_space=pltpu.VMEM), pl.BlockSpec(memory_space=pltpu.VMEM)),
        scratch_shapes=[pltpu.VMEM((tok_nq, 128), jnp.float32)],
        compiler_params=pltpu.CompilerParams(vmem_limit_bytes=24 * 1024 * 1024),
        cost_estimate=pl.CostEstimate(
            flops=2 * tok_nq * tok * no * width, transcendentals=0, bytes_accessed=(tok_nq + tok * no) * width * 2
        ),
    )(query, other_packed, query_valid)


def shards(encoded, slot_items, lengths, token_mask):
    n_enc = lax.axis_size("enc")
    n_pool = lax.axis_size("pool")
    owners = n_enc * n_pool
    group = encoded.shape[0]
    toks = encoded.shape[1]
    width = encoded.shape[2]
    items_dev = lengths.shape[0]
    per = items_dev // n_pool
    tok = n_enc * toks
    n_tok = items_dev * tok
    pool_index = lax.axis_index("pool")

    table = slot_items.reshape(owners, n_pool, per)
    mine = lax.dynamic_index_in_dim(table, pool_index, 1, keepdims=False) - pool_index * group
    outgoing = jnp.take(encoded, mine, axis=0, mode="clip")
    outgoing = jnp.transpose(outgoing, (2, 0, 1, 3))
    arrived = lax.all_to_all(outgoing, ("enc", "pool"), split_axis=1, concat_axis=1, tiled=True)
    slotted = arrived.reshape(tok, items_dev, width)
    values = slotted.astype(jnp.float32)
    normed = (values / jnp.sqrt(jnp.sum(values * values, axis=-1, keepdims=True) + 1e-06)).astype(
        jnp.bfloat16
    )
    position = jnp.arange(tok, dtype=jnp.int32)[None, :]
    valid = (position < lengths[:, None]) & ((position == 0) | (token_mask == 1))
    valid_tm = jnp.transpose(valid.reshape(items_dev, n_enc, toks), (2, 1, 0)).reshape(tok, items_dev)
    bias = jnp.where(valid_tm, 0.0, -4.0).astype(jnp.bfloat16)
    normed = jnp.where(valid_tm[:, :, None], normed, normed[0][None])
    packed = jnp.concatenate([normed.reshape(n_tok, width), bias.reshape(-1, width)], axis=0)
    block = packed[:n_tok].reshape(tok, items_dev, width)

    parity = (pool_index ^ (pool_index >> 1) ^ (pool_index >> 2)) & 1
    is_a = (pool_index & 1) == 0

    def par(p):
        return (p ^ (p >> 1) ^ (p >> 2)) & 1

    send_pairs = [(p, p ^ (4 if par(p) else 2)) for p in range(n_pool)]
    back_pairs = [(t, s) for s, t in send_pairs]
    chip_pairs = [(p, p ^ 1) for p in range(n_pool)]

    z_recv = lax.ppermute(packed, "pool", send_pairs)
    c_recv = lax.ppermute(packed, "pool", chip_pairs)

    def row_flags(valid_rows):
        return jnp.broadcast_to(valid_rows.astype(jnp.float32).reshape(-1, 1), (valid_rows.size, 128))

    half = items_dev // 2
    own_flags = row_flags(valid_tm)
    c_blk = c_recv[:n_tok].reshape(tok, items_dev, width)
    c_valid = c_recv[n_tok:].reshape(tok, items_dev) == 0
    query = jnp.where(is_a, block[:, :half], c_blk[:, half:]).reshape(tok * half, width)
    query_flags = row_flags(jnp.where(is_a, valid_tm[:, :half], c_valid[:, half:]))
    other_packed = jnp.where(is_a, c_recv, packed)
    part, _ = chamfer_tile(query, query_flags, other_packed, tok)
    part, own_flags = lax.optimization_barrier((part, own_flags))
    part_recv = lax.ppermute(part, "pool", chip_pairs)
    joined = jnp.where(
        is_a,
        jnp.concatenate([part, part_recv], axis=0),
        jnp.concatenate([part_recv, part], axis=0),
    )
    tile0 = jnp.where(is_a, joined, joined.T)

    tile_z, tile_z_t = chamfer_tile(block.reshape(n_tok, width), own_flags, z_recv, tok)
    tile_back = lax.ppermute(tile_z_t, "pool", back_pairs)
    ready = lax.optimization_barrier(jnp.concatenate([tile0, tile_z, tile_z], axis=1))
    column = jnp.arange(3 * items_dev, dtype=jnp.int32)[None, :] // items_dev
    return jnp.where(column == 1 + parity, jnp.tile(tile_back, (1, 3)), ready)


def solution(mesh):
    in_specs = (P("pool", "enc", None), P(), P(("enc", "pool")), P(("enc", "pool"), None))
    out_specs = P(("enc", "pool"), None)
    return jax.shard_map(shards, mesh=mesh, in_specs=in_specs, out_specs=out_specs, check_vma=False)
```

```python
import functools

import jax
import jax.numpy as jnp
from jax import lax
from jax.experimental import pallas as pl
from jax.experimental.pallas import tpu as pltpu
from jax.sharding import PartitionSpec as P


def tile_scores(query, query_bias, other, other_bias):
    tok, query_items, width = query.shape
    other_items = other.shape[1]
    rows = min(32, query_items)
    blocks = query_items // rows
    other_flat = other.reshape(tok * other_items, width)
    other_add = other_bias.astype(jnp.float32)[:, :, None]
    other_valid = other_bias == 0
    turned_all = jnp.transpose(query.reshape(tok, blocks, rows, width), (1, 0, 2, 3))
    adding_all = jnp.transpose(query_bias.astype(jnp.float32).reshape(tok, blocks, rows), (1, 0, 2))[..., None]
    kept_all = jnp.transpose((query_bias == 0).reshape(tok, blocks, rows), (1, 0, 2))

    def one_block(operands):
        turned, adding, kept = operands
        flat = turned.reshape(tok * rows, width)
        dots_fore = jnp.einsum("ubh,qh->ubq", other, flat, preferred_element_type=jnp.float32)
        fore = jnp.max(dots_fore + other_add, axis=0).reshape(other_items, tok, rows)
        fore = jnp.sum(jnp.where(kept[None], fore, 0.0), axis=1)
        dots_back = jnp.einsum("trh,ch->trc", turned, other_flat, preferred_element_type=jnp.float32)
        back = jnp.max(dots_back + adding, axis=0).reshape(rows, tok, other_items)
        back = jnp.sum(jnp.where(other_valid[None], back, 0.0), axis=1)
        return 0.5 * (fore.T + back)

    result = lax.map(one_block, (turned_all, adding_all, kept_all))
    return result.reshape(query_items, other_items)


def _chamfer_kernel(tok, nq, no, cw, q_ref, o_ref, qv_ref, out_ref, out_t_ref, fm_ref):
    q = q_ref[0:tok * nq, :]
    n_rows = tok * no // 128
    flags = o_ref[tok * no:tok * no + n_rows, :].astype(jnp.float32)
    acc_b = jnp.zeros((nq, 128), jnp.float32)
    for c in range(tok * no // cw):
        o_c = o_ref[c * cw:(c + 1) * cw, :]
        d = lax.dot_general(q, o_c, (((1,), (1,)), ((), ())), preferred_element_type=jnp.float32)
        m = d[:, 0:128]
        for k in range(1, cw // 128):
            m = jnp.maximum(m, d[:, k * 128:(k + 1) * 128])
        if c == 0:
            fm_ref[...] = m
        else:
            fm_ref[...] = jnp.maximum(fm_ref[...], m)
        mb = jnp.max(d.reshape(tok, nq, cw), axis=0)
        for k in range(cw // 128):
            row = c * (cw // 128) + k
            acc_b = acc_b + jnp.where(flags[row:row + 1, :] == 0, mb[:, k * 128:(k + 1) * 128], 0.0)
    fm = fm_ref[...]
    fm = jnp.maximum(fm, pltpu.roll(fm, 64, 1))
    fsum = jnp.sum(jnp.where(qv_ref[...] > 0, fm, 0.0).reshape(tok, nq, 128), axis=0)
    bsum = acc_b + pltpu.roll(acc_b, 64, 1)
    res = 0.5 * (fsum + bsum)
    out_ref[...] = res[:, :no]
    out_t_ref[...] = res.T[:no, :]


def chamfer_tile(query, query_valid, other_packed, tok):
    tok_nq, width = query_valid.shape[0], query.shape[1]
    nq = tok_nq // tok
    no = 64
    cw = 512
    kernel = functools.partial(_chamfer_kernel, tok, nq, no, cw)
    return pl.pallas_call(
        kernel,
        out_shape=(jax.ShapeDtypeStruct((nq, no), jnp.float32), jax.ShapeDtypeStruct((no, nq), jnp.float32)),
        in_specs=[pl.BlockSpec(memory_space=pltpu.VMEM)] * 3,
        out_specs=(pl.BlockSpec(memory_space=pltpu.VMEM), pl.BlockSpec(memory_space=pltpu.VMEM)),
        scratch_shapes=[pltpu.VMEM((tok_nq, 128), jnp.float32)],
        compiler_params=pltpu.CompilerParams(vmem_limit_bytes=24 * 1024 * 1024),
        cost_estimate=pl.CostEstimate(
            flops=2 * tok_nq * tok * no * width, transcendentals=0, bytes_accessed=(tok_nq + tok * no) * width * 2
        ),
    )(query, other_packed, query_valid)


def shards(encoded, slot_items, lengths, token_mask):
    n_enc = lax.axis_size("enc")
    n_pool = lax.axis_size("pool")
    owners = n_enc * n_pool
    group = encoded.shape[0]
    toks = encoded.shape[1]
    width = encoded.shape[2]
    items_dev = lengths.shape[0]
    per = items_dev // n_pool
    tok = n_enc * toks
    n_tok = items_dev * tok
    pool_index = lax.axis_index("pool")

    table = slot_items.reshape(owners, n_pool, per)
    mine = lax.dynamic_index_in_dim(table, pool_index, 1, keepdims=False) - pool_index * group
    outgoing = jnp.take(encoded, mine, axis=0, mode="clip")
    outgoing = jnp.transpose(outgoing, (2, 0, 1, 3))
    arrived = lax.all_to_all(outgoing, ("enc", "pool"), split_axis=1, concat_axis=1, tiled=True)
    slotted = arrived.reshape(tok, items_dev, width)
    values = slotted.astype(jnp.float32)
    normed = (values / jnp.sqrt(jnp.sum(values * values, axis=-1, keepdims=True) + 1e-06)).astype(
        jnp.bfloat16
    )
    position = jnp.arange(tok, dtype=jnp.int32)[None, :]
    valid = (position < lengths[:, None]) & ((position == 0) | (token_mask == 1))
    valid_tm = jnp.transpose(valid.reshape(items_dev, n_enc, toks), (2, 1, 0)).reshape(tok, items_dev)
    bias = jnp.where(valid_tm, 0.0, -4.0).astype(jnp.bfloat16)
    normed = jnp.where(valid_tm[:, :, None], normed, normed[0][None])
    packed = jnp.concatenate([normed.reshape(n_tok, width), bias.reshape(-1, width)], axis=0)
    block = packed[:n_tok].reshape(tok, items_dev, width)

    parity = (pool_index ^ (pool_index >> 1) ^ (pool_index >> 2)) & 1
    is_a = (pool_index & 1) == 0

    def par(p):
        return (p ^ (p >> 1) ^ (p >> 2)) & 1

    send_pairs = [(p, p ^ (4 if par(p) else 2)) for p in range(n_pool)]
    back_pairs = [(t, s) for s, t in send_pairs]
    chip_pairs = [(p, p ^ 1) for p in range(n_pool)]

    z_recv = lax.ppermute(packed, "pool", send_pairs)
    c_recv = lax.ppermute(packed, "pool", chip_pairs)

    def row_flags(valid_rows):
        return jnp.broadcast_to(valid_rows.astype(jnp.float32).reshape(-1, 1), (valid_rows.size, 128))

    half = items_dev // 2
    own_flags = row_flags(valid_tm)
    c_blk = c_recv[:n_tok].reshape(tok, items_dev, width)
    c_valid = c_recv[n_tok:].reshape(tok, items_dev) == 0
    query = jnp.where(is_a, block[:, :half], c_blk[:, half:]).reshape(tok * half, width)
    query_flags = row_flags(jnp.where(is_a, valid_tm[:, :half], c_valid[:, half:]))
    other_packed = jnp.where(is_a, c_recv, packed)
    part, _ = chamfer_tile(query, query_flags, other_packed, tok)
    part, own_flags = lax.optimization_barrier((part, own_flags))
    part_recv = lax.ppermute(part, "pool", chip_pairs)
    joined = jnp.where(
        is_a,
        jnp.concatenate([part, part_recv], axis=0),
        jnp.concatenate([part_recv, part], axis=0),
    )
    tile0 = jnp.where(is_a, joined, joined.T)

    tile_z, tile_z_t = chamfer_tile(packed, own_flags, z_recv, tok)
    tile_back = lax.ppermute(tile_z_t, "pool", back_pairs)
    ready = lax.optimization_barrier(jnp.concatenate([tile0, tile_z, tile_z], axis=1))
    column = jnp.arange(3 * items_dev, dtype=jnp.int32)[None, :] // items_dev
    return jnp.where(column == 1 + parity, jnp.tile(tile_back, (1, 3)), ready)


def solution(mesh):
    in_specs = (P("pool", "enc", None), P(), P(("enc", "pool")), P(("enc", "pool"), None))
    out_specs = P(("enc", "pool"), None)
    return jax.shard_map(shards, mesh=mesh, in_specs=in_specs, out_specs=out_specs, check_vma=False)
```

```python
import functools

import jax
import jax.numpy as jnp
from jax import lax
from jax.experimental import pallas as pl
from jax.experimental.pallas import tpu as pltpu
from jax.sharding import PartitionSpec as P


def tile_scores(query, query_bias, other, other_bias):
    tok, query_items, width = query.shape
    other_items = other.shape[1]
    rows = min(32, query_items)
    blocks = query_items // rows
    other_flat = other.reshape(tok * other_items, width)
    other_add = other_bias.astype(jnp.float32)[:, :, None]
    other_valid = other_bias == 0
    turned_all = jnp.transpose(query.reshape(tok, blocks, rows, width), (1, 0, 2, 3))
    adding_all = jnp.transpose(query_bias.astype(jnp.float32).reshape(tok, blocks, rows), (1, 0, 2))[..., None]
    kept_all = jnp.transpose((query_bias == 0).reshape(tok, blocks, rows), (1, 0, 2))

    def one_block(operands):
        turned, adding, kept = operands
        flat = turned.reshape(tok * rows, width)
        dots_fore = jnp.einsum("ubh,qh->ubq", other, flat, preferred_element_type=jnp.float32)
        fore = jnp.max(dots_fore + other_add, axis=0).reshape(other_items, tok, rows)
        fore = jnp.sum(jnp.where(kept[None], fore, 0.0), axis=1)
        dots_back = jnp.einsum("trh,ch->trc", turned, other_flat, preferred_element_type=jnp.float32)
        back = jnp.max(dots_back + adding, axis=0).reshape(rows, tok, other_items)
        back = jnp.sum(jnp.where(other_valid[None], back, 0.0), axis=1)
        return 0.5 * (fore.T + back)

    result = lax.map(one_block, (turned_all, adding_all, kept_all))
    return result.reshape(query_items, other_items)


def _chamfer_kernel(tok, nq, no, cw, q_ref, o_ref, qv_ref, out_ref, out_t_ref, fm_ref):
    q = q_ref[0:tok * nq, :]
    n_rows = tok * no // 128
    flags = o_ref[tok * no:tok * no + n_rows, :].astype(jnp.float32)
    acc_b = jnp.zeros((nq, 128), jnp.float32)
    for c in range(tok * no // cw):
        o_c = o_ref[c * cw:(c + 1) * cw, :]
        d = lax.dot_general(q, o_c, (((1,), (1,)), ((), ())), preferred_element_type=jnp.float32)
        m = d[:, 0:128]
        for k in range(1, cw // 128):
            m = jnp.maximum(m, d[:, k * 128:(k + 1) * 128])
        if c == 0:
            fm_ref[...] = m
        else:
            fm_ref[...] = jnp.maximum(fm_ref[...], m)
        mb = jnp.max(d.reshape(tok, nq, cw), axis=0)
        for k in range(cw // 128):
            row = c * (cw // 128) + k
            acc_b = acc_b + jnp.where(flags[row:row + 1, :] == 0, mb[:, k * 128:(k + 1) * 128], 0.0)
    fm = fm_ref[...]
    fm = jnp.maximum(fm, pltpu.roll(fm, 64, 1))
    fsum = jnp.sum(jnp.where(qv_ref[...] > 0, fm, 0.0).reshape(tok, nq, 128), axis=0)
    bsum = acc_b + pltpu.roll(acc_b, 64, 1)
    res = 0.5 * (fsum + bsum)
    out_ref[...] = res[:, :no]
    out_t_ref[...] = res.T[:no, :]


def chamfer_tile(query, query_valid, other_packed, tok):
    tok_nq, width = query_valid.shape[0], query.shape[1]
    nq = tok_nq // tok
    no = 64
    cw = 512
    kernel = functools.partial(_chamfer_kernel, tok, nq, no, cw)
    return pl.pallas_call(
        kernel,
        out_shape=(jax.ShapeDtypeStruct((nq, no), jnp.float32), jax.ShapeDtypeStruct((no, nq), jnp.float32)),
        in_specs=[pl.BlockSpec(memory_space=pltpu.VMEM)] * 3,
        out_specs=(pl.BlockSpec(memory_space=pltpu.VMEM), pl.BlockSpec(memory_space=pltpu.VMEM)),
        scratch_shapes=[pltpu.VMEM((tok_nq, 128), jnp.float32)],
        compiler_params=pltpu.CompilerParams(vmem_limit_bytes=24 * 1024 * 1024),
        cost_estimate=pl.CostEstimate(
            flops=2 * tok_nq * tok * no * width, transcendentals=0, bytes_accessed=(tok_nq + tok * no) * width * 2
        ),
    )(query, other_packed, query_valid)


def shards(encoded, slot_items, lengths, token_mask):
    n_enc = lax.axis_size("enc")
    n_pool = lax.axis_size("pool")
    owners = n_enc * n_pool
    group = encoded.shape[0]
    toks = encoded.shape[1]
    width = encoded.shape[2]
    items_dev = lengths.shape[0]
    per = items_dev // n_pool
    tok = n_enc * toks
    n_tok = items_dev * tok
    pool_index = lax.axis_index("pool")

    table = slot_items.reshape(owners, n_pool, per)
    mine = lax.dynamic_index_in_dim(table, pool_index, 1, keepdims=False) - pool_index * group
    outgoing = jnp.take(encoded, mine, axis=0, mode="clip")
    outgoing = jnp.transpose(outgoing, (2, 0, 1, 3))
    arrived = lax.all_to_all(outgoing, ("enc", "pool"), split_axis=1, concat_axis=1, tiled=True)
    slotted = arrived.reshape(tok, items_dev, width)
    position = jnp.arange(tok, dtype=jnp.int32)[None, :]
    valid = (position < lengths[:, None]) & ((position == 0) | (token_mask == 1))
    valid_tm = jnp.transpose(valid.reshape(items_dev, n_enc, toks), (2, 1, 0)).reshape(tok, items_dev)
    bias = jnp.where(valid_tm, 0.0, -4.0).astype(jnp.bfloat16)
    slotted = jnp.where(valid_tm[:, :, None], slotted, slotted[0][None])
    values = slotted.astype(jnp.float32)
    normed = (values / jnp.sqrt(jnp.sum(values * values, axis=-1, keepdims=True) + 1e-06)).astype(
        jnp.bfloat16
    )
    packed = jnp.concatenate([normed.reshape(n_tok, width), bias.reshape(-1, width)], axis=0)
    block = packed[:n_tok].reshape(tok, items_dev, width)

    parity = (pool_index ^ (pool_index >> 1) ^ (pool_index >> 2)) & 1
    is_a = (pool_index & 1) == 0

    def par(p):
        return (p ^ (p >> 1) ^ (p >> 2)) & 1

    send_pairs = [(p, p ^ (4 if par(p) else 2)) for p in range(n_pool)]
    back_pairs = [(t, s) for s, t in send_pairs]
    chip_pairs = [(p, p ^ 1) for p in range(n_pool)]

    z_recv = lax.ppermute(packed, "pool", send_pairs)
    c_recv = lax.ppermute(packed, "pool", chip_pairs)

    def row_flags(valid_rows):
        return jnp.broadcast_to(valid_rows.astype(jnp.float32).reshape(-1, 1), (valid_rows.size, 128))

    half = items_dev // 2
    own_flags = row_flags(valid_tm)
    c_blk = c_recv[:n_tok].reshape(tok, items_dev, width)
    c_valid = c_recv[n_tok:].reshape(tok, items_dev) == 0
    query = jnp.where(is_a, block[:, :half], c_blk[:, half:]).reshape(tok * half, width)
    query_flags = row_flags(jnp.where(is_a, valid_tm[:, :half], c_valid[:, half:]))
    other_packed = jnp.where(is_a, c_recv, packed)
    part, _ = chamfer_tile(query, query_flags, other_packed, tok)
    part, own_flags = lax.optimization_barrier((part, own_flags))
    part_recv = lax.ppermute(part, "pool", chip_pairs)
    joined = jnp.where(
        is_a,
        jnp.concatenate([part, part_recv], axis=0),
        jnp.concatenate([part_recv, part], axis=0),
    )
    tile0 = jnp.where(is_a, joined, joined.T)

    tile_z, tile_z_t = chamfer_tile(packed, own_flags, z_recv, tok)
    tile_back = lax.ppermute(tile_z_t, "pool", back_pairs)
    ready = lax.optimization_barrier(jnp.concatenate([tile0, tile_z, tile_z], axis=1))
    column = jnp.arange(3 * items_dev, dtype=jnp.int32)[None, :] // items_dev
    return jnp.where(column == 1 + parity, jnp.tile(tile_back, (1, 3)), ready)


def solution(mesh):
    in_specs = (P("pool", "enc", None), P(), P(("enc", "pool")), P(("enc", "pool"), None))
    out_specs = P(("enc", "pool"), None)
    return jax.shard_map(shards, mesh=mesh, in_specs=in_specs, out_specs=out_specs, check_vma=False)
```

```python
import functools

import jax
import jax.numpy as jnp
from jax import lax
from jax.experimental import pallas as pl
from jax.experimental.pallas import tpu as pltpu
from jax.sharding import PartitionSpec as P


def tile_scores(query, query_bias, other, other_bias):
    tok, query_items, width = query.shape
    other_items = other.shape[1]
    rows = min(32, query_items)
    blocks = query_items // rows
    other_flat = other.reshape(tok * other_items, width)
    other_add = other_bias.astype(jnp.float32)[:, :, None]
    other_valid = other_bias == 0
    turned_all = jnp.transpose(query.reshape(tok, blocks, rows, width), (1, 0, 2, 3))
    adding_all = jnp.transpose(query_bias.astype(jnp.float32).reshape(tok, blocks, rows), (1, 0, 2))[..., None]
    kept_all = jnp.transpose((query_bias == 0).reshape(tok, blocks, rows), (1, 0, 2))

    def one_block(operands):
        turned, adding, kept = operands
        flat = turned.reshape(tok * rows, width)
        dots_fore = jnp.einsum("ubh,qh->ubq", other, flat, preferred_element_type=jnp.float32)
        fore = jnp.max(dots_fore + other_add, axis=0).reshape(other_items, tok, rows)
        fore = jnp.sum(jnp.where(kept[None], fore, 0.0), axis=1)
        dots_back = jnp.einsum("trh,ch->trc", turned, other_flat, preferred_element_type=jnp.float32)
        back = jnp.max(dots_back + adding, axis=0).reshape(rows, tok, other_items)
        back = jnp.sum(jnp.where(other_valid[None], back, 0.0), axis=1)
        return 0.5 * (fore.T + back)

    result = lax.map(one_block, (turned_all, adding_all, kept_all))
    return result.reshape(query_items, other_items)


def _chamfer_kernel(tok, nq, no, cw, q_ref, o_ref, qv_ref, out_ref, out_t_ref, fm_ref):
    q = q_ref[0:tok * nq, :]
    n_rows = tok * no // 128
    flags = o_ref[tok * no:tok * no + n_rows, :].astype(jnp.float32)
    acc_b = jnp.zeros((nq, 128), jnp.float32)
    for c in range(tok * no // cw):
        o_c = o_ref[c * cw:(c + 1) * cw, :]
        d = lax.dot_general(q, o_c, (((1,), (1,)), ((), ())), preferred_element_type=jnp.float32)
        m = d[:, 0:128]
        for k in range(1, cw // 128):
            m = jnp.maximum(m, d[:, k * 128:(k + 1) * 128])
        if c == 0:
            fm_ref[...] = m
        else:
            fm_ref[...] = jnp.maximum(fm_ref[...], m)
        mb = jnp.max(d.reshape(tok, nq, cw), axis=0)
        for k in range(cw // 128):
            row = c * (cw // 128) + k
            acc_b = acc_b + jnp.where(flags[row:row + 1, :] == 0, mb[:, k * 128:(k + 1) * 128], 0.0)
    fm = fm_ref[...]
    fm = jnp.maximum(fm, pltpu.roll(fm, 64, 1))
    fsum = jnp.sum(jnp.where(qv_ref[...] > 0, fm, 0.0).reshape(tok, nq, 128), axis=0)
    bsum = acc_b + pltpu.roll(acc_b, 64, 1)
    res = 0.5 * (fsum + bsum)
    out_ref[...] = res[:, :no]
    out_t_ref[...] = res.T[:no, :]


def chamfer_tile(query, query_valid, other_packed, tok):
    tok_nq, width = query_valid.shape[0], query.shape[1]
    nq = tok_nq // tok
    no = 64
    cw = 1024
    kernel = functools.partial(_chamfer_kernel, tok, nq, no, cw)
    return pl.pallas_call(
        kernel,
        out_shape=(jax.ShapeDtypeStruct((nq, no), jnp.float32), jax.ShapeDtypeStruct((no, nq), jnp.float32)),
        in_specs=[pl.BlockSpec(memory_space=pltpu.VMEM)] * 3,
        out_specs=(pl.BlockSpec(memory_space=pltpu.VMEM), pl.BlockSpec(memory_space=pltpu.VMEM)),
        scratch_shapes=[pltpu.VMEM((tok_nq, 128), jnp.float32)],
        compiler_params=pltpu.CompilerParams(vmem_limit_bytes=24 * 1024 * 1024),
        cost_estimate=pl.CostEstimate(
            flops=2 * tok_nq * tok * no * width, transcendentals=0, bytes_accessed=(tok_nq + tok * no) * width * 2
        ),
    )(query, other_packed, query_valid)


def shards(encoded, slot_items, lengths, token_mask):
    n_enc = lax.axis_size("enc")
    n_pool = lax.axis_size("pool")
    owners = n_enc * n_pool
    group = encoded.shape[0]
    toks = encoded.shape[1]
    width = encoded.shape[2]
    items_dev = lengths.shape[0]
    per = items_dev // n_pool
    tok = n_enc * toks
    n_tok = items_dev * tok
    pool_index = lax.axis_index("pool")

    table = slot_items.reshape(owners, n_pool, per)
    mine = lax.dynamic_index_in_dim(table, pool_index, 1, keepdims=False) - pool_index * group
    outgoing = jnp.take(encoded, mine, axis=0, mode="clip")
    outgoing = jnp.transpose(outgoing, (2, 0, 1, 3))
    arrived = lax.all_to_all(outgoing, ("enc", "pool"), split_axis=1, concat_axis=1, tiled=True)
    slotted = arrived.reshape(tok, items_dev, width)
    values = slotted.astype(jnp.float32)
    normed = (values / jnp.sqrt(jnp.sum(values * values, axis=-1, keepdims=True) + 1e-06)).astype(
        jnp.bfloat16
    )
    position = jnp.arange(tok, dtype=jnp.int32)[None, :]
    valid = (position < lengths[:, None]) & ((position == 0) | (token_mask == 1))
    valid_tm = jnp.transpose(valid.reshape(items_dev, n_enc, toks), (2, 1, 0)).reshape(tok, items_dev)
    bias = jnp.where(valid_tm, 0.0, -4.0).astype(jnp.bfloat16)
    normed = jnp.where(valid_tm[:, :, None], normed, normed[0][None])
    packed = jnp.concatenate([normed.reshape(n_tok, width), bias.reshape(-1, width)], axis=0)
    block = packed[:n_tok].reshape(tok, items_dev, width)

    parity = (pool_index ^ (pool_index >> 1) ^ (pool_index >> 2)) & 1
    is_a = (pool_index & 1) == 0

    def par(p):
        return (p ^ (p >> 1) ^ (p >> 2)) & 1

    send_pairs = [(p, p ^ (4 if par(p) else 2)) for p in range(n_pool)]
    back_pairs = [(t, s) for s, t in send_pairs]
    chip_pairs = [(p, p ^ 1) for p in range(n_pool)]

    z_recv = lax.ppermute(packed, "pool", send_pairs)
    c_recv = lax.ppermute(packed, "pool", chip_pairs)

    def row_flags(valid_rows):
        return jnp.broadcast_to(valid_rows.astype(jnp.float32).reshape(-1, 1), (valid_rows.size, 128))

    half = items_dev // 2
    own_flags = row_flags(valid_tm)
    c_blk = c_recv[:n_tok].reshape(tok, items_dev, width)
    c_valid = c_recv[n_tok:].reshape(tok, items_dev) == 0
    query = jnp.where(is_a, block[:, :half], c_blk[:, half:]).reshape(tok * half, width)
    query_flags = row_flags(jnp.where(is_a, valid_tm[:, :half], c_valid[:, half:]))
    other_packed = jnp.where(is_a, c_recv, packed)
    part, _ = chamfer_tile(query, query_flags, other_packed, tok)
    part, own_flags = lax.optimization_barrier((part, own_flags))
    part_recv = lax.ppermute(part, "pool", chip_pairs)
    joined = jnp.where(
        is_a,
        jnp.concatenate([part, part_recv], axis=0),
        jnp.concatenate([part_recv, part], axis=0),
    )
    tile0 = jnp.where(is_a, joined, joined.T)

    tile_z, tile_z_t = chamfer_tile(packed, own_flags, z_recv, tok)
    tile_back = lax.ppermute(tile_z_t, "pool", back_pairs)
    ready = lax.optimization_barrier(jnp.concatenate([tile0, tile_z, tile_z], axis=1))
    column = jnp.arange(3 * items_dev, dtype=jnp.int32)[None, :] // items_dev
    return jnp.where(column == 1 + parity, jnp.tile(tile_back, (1, 3)), ready)


def solution(mesh):
    in_specs = (P("pool", "enc", None), P(), P(("enc", "pool")), P(("enc", "pool"), None))
    out_specs = P(("enc", "pool"), None)
    return jax.shard_map(shards, mesh=mesh, in_specs=in_specs, out_specs=out_specs, check_vma=False)
```

```python
import functools

import jax
import jax.numpy as jnp
from jax import lax
from jax.experimental import pallas as pl
from jax.experimental.pallas import tpu as pltpu
from jax.sharding import PartitionSpec as P


def tile_scores(query, query_bias, other, other_bias):
    tok, query_items, width = query.shape
    other_items = other.shape[1]
    rows = min(32, query_items)
    blocks = query_items // rows
    other_flat = other.reshape(tok * other_items, width)
    other_add = other_bias.astype(jnp.float32)[:, :, None]
    other_valid = other_bias == 0
    turned_all = jnp.transpose(query.reshape(tok, blocks, rows, width), (1, 0, 2, 3))
    adding_all = jnp.transpose(query_bias.astype(jnp.float32).reshape(tok, blocks, rows), (1, 0, 2))[..., None]
    kept_all = jnp.transpose((query_bias == 0).reshape(tok, blocks, rows), (1, 0, 2))

    def one_block(operands):
        turned, adding, kept = operands
        flat = turned.reshape(tok * rows, width)
        dots_fore = jnp.einsum("ubh,qh->ubq", other, flat, preferred_element_type=jnp.float32)
        fore = jnp.max(dots_fore + other_add, axis=0).reshape(other_items, tok, rows)
        fore = jnp.sum(jnp.where(kept[None], fore, 0.0), axis=1)
        dots_back = jnp.einsum("trh,ch->trc", turned, other_flat, preferred_element_type=jnp.float32)
        back = jnp.max(dots_back + adding, axis=0).reshape(rows, tok, other_items)
        back = jnp.sum(jnp.where(other_valid[None], back, 0.0), axis=1)
        return 0.5 * (fore.T + back)

    result = lax.map(one_block, (turned_all, adding_all, kept_all))
    return result.reshape(query_items, other_items)


def _chamfer_kernel(tok, nq, no, cw, q_ref, o_ref, qv_ref, out_ref, out_t_ref, fm_ref):
    q = q_ref[0:tok * nq, :]
    n_rows = tok * no // 128
    flags = o_ref[tok * no:tok * no + n_rows, :].astype(jnp.float32)
    acc_b = jnp.zeros((nq, 128), jnp.float32)
    for c in range(tok * no // cw):
        o_c = o_ref[c * cw:(c + 1) * cw, :]
        d = lax.dot_general(q, o_c, (((1,), (1,)), ((), ())), preferred_element_type=jnp.float32)
        m = d[:, 0:128]
        for k in range(1, cw // 128):
            m = jnp.maximum(m, d[:, k * 128:(k + 1) * 128])
        if c == 0:
            fm_ref[...] = m
        else:
            fm_ref[...] = jnp.maximum(fm_ref[...], m)
        mb = jnp.max(d.reshape(tok, nq, cw), axis=0)
        for k in range(cw // 128):
            row = c * (cw // 128) + k
            acc_b = acc_b + jnp.where(flags[row:row + 1, :] == 0, mb[:, k * 128:(k + 1) * 128], 0.0)
    fm = fm_ref[...]
    fm = jnp.maximum(fm, pltpu.roll(fm, 64, 1))
    fsum = jnp.sum(jnp.where(qv_ref[...] > 0, fm, 0.0).reshape(tok, nq, 128), axis=0)
    bsum = acc_b + pltpu.roll(acc_b, 64, 1)
    res = 0.5 * (fsum + bsum)
    out_ref[...] = res[:, :no]
    out_t_ref[...] = res.T[:no, :]


def chamfer_tile(query, query_valid, other_packed, tok):
    tok_nq, width = query_valid.shape[0], query.shape[1]
    nq = tok_nq // tok
    no = 64
    cw = 256
    kernel = functools.partial(_chamfer_kernel, tok, nq, no, cw)
    return pl.pallas_call(
        kernel,
        out_shape=(jax.ShapeDtypeStruct((nq, no), jnp.float32), jax.ShapeDtypeStruct((no, nq), jnp.float32)),
        in_specs=[pl.BlockSpec(memory_space=pltpu.VMEM)] * 3,
        out_specs=(pl.BlockSpec(memory_space=pltpu.VMEM), pl.BlockSpec(memory_space=pltpu.VMEM)),
        scratch_shapes=[pltpu.VMEM((tok_nq, 128), jnp.float32)],
        compiler_params=pltpu.CompilerParams(vmem_limit_bytes=24 * 1024 * 1024),
        cost_estimate=pl.CostEstimate(
            flops=2 * tok_nq * tok * no * width, transcendentals=0, bytes_accessed=(tok_nq + tok * no) * width * 2
        ),
    )(query, other_packed, query_valid)


def shards(encoded, slot_items, lengths, token_mask):
    n_enc = lax.axis_size("enc")
    n_pool = lax.axis_size("pool")
    owners = n_enc * n_pool
    group = encoded.shape[0]
    toks = encoded.shape[1]
    width = encoded.shape[2]
    items_dev = lengths.shape[0]
    per = items_dev // n_pool
    tok = n_enc * toks
    n_tok = items_dev * tok
    pool_index = lax.axis_index("pool")

    table = slot_items.reshape(owners, n_pool, per)
    mine = lax.dynamic_index_in_dim(table, pool_index, 1, keepdims=False) - pool_index * group
    outgoing = jnp.take(encoded, mine, axis=0, mode="clip")
    outgoing = jnp.transpose(outgoing, (2, 0, 1, 3))
    arrived = lax.all_to_all(outgoing, ("enc", "pool"), split_axis=1, concat_axis=1, tiled=True)
    slotted = arrived.reshape(tok, items_dev, width)
    values = slotted.astype(jnp.float32)
    normed = (values / jnp.sqrt(jnp.sum(values * values, axis=-1, keepdims=True) + 1e-06)).astype(
        jnp.bfloat16
    )
    position = jnp.arange(tok, dtype=jnp.int32)[None, :]
    valid = (position < lengths[:, None]) & ((position == 0) | (token_mask == 1))
    valid_tm = jnp.transpose(valid.reshape(items_dev, n_enc, toks), (2, 1, 0)).reshape(tok, items_dev)
    bias = jnp.where(valid_tm, 0.0, -4.0).astype(jnp.bfloat16)
    normed = jnp.where(valid_tm[:, :, None], normed, normed[0][None])
    packed = jnp.concatenate([normed.reshape(n_tok, width), bias.reshape(-1, width)], axis=0)
    block = packed[:n_tok].reshape(tok, items_dev, width)

    parity = (pool_index ^ (pool_index >> 1) ^ (pool_index >> 2)) & 1
    is_a = (pool_index & 1) == 0

    def par(p):
        return (p ^ (p >> 1) ^ (p >> 2)) & 1

    send_pairs = [(p, p ^ (4 if par(p) else 2)) for p in range(n_pool)]
    back_pairs = [(t, s) for s, t in send_pairs]
    chip_pairs = [(p, p ^ 1) for p in range(n_pool)]

    z_recv = lax.ppermute(packed, "pool", send_pairs)
    c_recv = lax.ppermute(packed, "pool", chip_pairs)

    def row_flags(valid_rows):
        return jnp.broadcast_to(valid_rows.astype(jnp.float32).reshape(-1, 1), (valid_rows.size, 128))

    half = items_dev // 2
    own_flags = row_flags(valid_tm)
    c_blk = c_recv[:n_tok].reshape(tok, items_dev, width)
    c_valid = c_recv[n_tok:].reshape(tok, items_dev) == 0
    query = jnp.where(is_a, block[:, :half], c_blk[:, half:]).reshape(tok * half, width)
    query_flags = row_flags(jnp.where(is_a, valid_tm[:, :half], c_valid[:, half:]))
    other_packed = jnp.where(is_a, c_recv, packed)
    part, _ = chamfer_tile(query, query_flags, other_packed, tok)
    part, own_flags = lax.optimization_barrier((part, own_flags))
    part_recv = lax.ppermute(part, "pool", chip_pairs)
    joined = jnp.where(
        is_a,
        jnp.concatenate([part, part_recv], axis=0),
        jnp.concatenate([part_recv, part], axis=0),
    )
    tile0 = jnp.where(is_a, joined, joined.T)

    tile_z, tile_z_t = chamfer_tile(packed, own_flags, z_recv, tok)
    tile_back = lax.ppermute(tile_z_t, "pool", back_pairs)
    ready = lax.optimization_barrier(jnp.concatenate([tile0, tile_z, tile_z], axis=1))
    column = jnp.arange(3 * items_dev, dtype=jnp.int32)[None, :] // items_dev
    return jnp.where(column == 1 + parity, jnp.tile(tile_back, (1, 3)), ready)


def solution(mesh):
    in_specs = (P("pool", "enc", None), P(), P(("enc", "pool")), P(("enc", "pool"), None))
    out_specs = P(("enc", "pool"), None)
    return jax.shard_map(shards, mesh=mesh, in_specs=in_specs, out_specs=out_specs, check_vma=False)
```

```python
import functools

import jax
import jax.numpy as jnp
from jax import lax
from jax.experimental import pallas as pl
from jax.experimental.pallas import tpu as pltpu
from jax.sharding import PartitionSpec as P


def tile_scores(query, query_bias, other, other_bias):
    tok, query_items, width = query.shape
    other_items = other.shape[1]
    rows = min(32, query_items)
    blocks = query_items // rows
    other_flat = other.reshape(tok * other_items, width)
    other_add = other_bias.astype(jnp.float32)[:, :, None]
    other_valid = other_bias == 0
    turned_all = jnp.transpose(query.reshape(tok, blocks, rows, width), (1, 0, 2, 3))
    adding_all = jnp.transpose(query_bias.astype(jnp.float32).reshape(tok, blocks, rows), (1, 0, 2))[..., None]
    kept_all = jnp.transpose((query_bias == 0).reshape(tok, blocks, rows), (1, 0, 2))

    def one_block(operands):
        turned, adding, kept = operands
        flat = turned.reshape(tok * rows, width)
        dots_fore = jnp.einsum("ubh,qh->ubq", other, flat, preferred_element_type=jnp.float32)
        fore = jnp.max(dots_fore + other_add, axis=0).reshape(other_items, tok, rows)
        fore = jnp.sum(jnp.where(kept[None], fore, 0.0), axis=1)
        dots_back = jnp.einsum("trh,ch->trc", turned, other_flat, preferred_element_type=jnp.float32)
        back = jnp.max(dots_back + adding, axis=0).reshape(rows, tok, other_items)
        back = jnp.sum(jnp.where(other_valid[None], back, 0.0), axis=1)
        return 0.5 * (fore.T + back)

    result = lax.map(one_block, (turned_all, adding_all, kept_all))
    return result.reshape(query_items, other_items)


def _chamfer_kernel(tok, nq, no, cw, q_ref, o_ref, qv_ref, out_ref, out_t_ref, fm_ref):
    q = q_ref[0:tok * nq, :]
    n_rows = tok * no // 128
    flags = o_ref[tok * no:tok * no + n_rows, :].astype(jnp.float32)
    acc_b = jnp.zeros((nq, 128), jnp.float32)
    for c in range(tok * no // cw):
        o_c = o_ref[c * cw:(c + 1) * cw, :]
        d = lax.dot_general(q, o_c, (((1,), (1,)), ((), ())), preferred_element_type=jnp.float32)
        m = d[:, 0:128]
        for k in range(1, cw // 128):
            m = jnp.maximum(m, d[:, k * 128:(k + 1) * 128])
        if c == 0:
            fm_ref[...] = m
        else:
            fm_ref[...] = jnp.maximum(fm_ref[...], m)
        mb = jnp.max(d.reshape(tok, nq, cw), axis=0)
        for k in range(cw // 128):
            row = c * (cw // 128) + k
            acc_b = acc_b + jnp.where(flags[row:row + 1, :] == 0, mb[:, k * 128:(k + 1) * 128], 0.0)
    fm = fm_ref[...]
    fm = jnp.maximum(fm, pltpu.roll(fm, 64, 1))
    fsum = jnp.sum(jnp.where(qv_ref[...] > 0, fm, 0.0).reshape(tok, nq, 128), axis=0)
    bsum = acc_b + pltpu.roll(acc_b, 64, 1)
    res = 0.5 * (fsum + bsum)
    out_ref[...] = res[:, :no]
    out_t_ref[...] = res.T[:no, :]


def chamfer_tile(query, query_valid, other_packed, tok):
    tok_nq, width = query_valid.shape[0], query.shape[1]
    nq = tok_nq // tok
    no = 64
    cw = 512
    kernel = functools.partial(_chamfer_kernel, tok, nq, no, cw)
    return pl.pallas_call(
        kernel,
        out_shape=(jax.ShapeDtypeStruct((nq, no), jnp.float32), jax.ShapeDtypeStruct((no, nq), jnp.float32)),
        in_specs=[pl.BlockSpec(memory_space=pltpu.VMEM)] * 3,
        out_specs=(pl.BlockSpec(memory_space=pltpu.VMEM), pl.BlockSpec(memory_space=pltpu.VMEM)),
        scratch_shapes=[pltpu.VMEM((tok_nq, 128), jnp.float32)],
        compiler_params=pltpu.CompilerParams(vmem_limit_bytes=24 * 1024 * 1024),
        cost_estimate=pl.CostEstimate(
            flops=2 * tok_nq * tok * no * width, transcendentals=0, bytes_accessed=(tok_nq + tok * no) * width * 2
        ),
    )(query, other_packed, query_valid)


def shards(encoded, slot_items, lengths, token_mask):
    n_enc = lax.axis_size("enc")
    n_pool = lax.axis_size("pool")
    owners = n_enc * n_pool
    group = encoded.shape[0]
    toks = encoded.shape[1]
    width = encoded.shape[2]
    items_dev = lengths.shape[0]
    per = items_dev // n_pool
    tok = n_enc * toks
    n_tok = items_dev * tok
    pool_index = lax.axis_index("pool")

    table = slot_items.reshape(owners, n_pool, per)
    mine = lax.dynamic_index_in_dim(table, pool_index, 1, keepdims=False) - pool_index * group
    outgoing = jnp.take(encoded, mine, axis=0, mode="clip")
    outgoing = jnp.transpose(outgoing, (2, 0, 1, 3))
    arrived = lax.all_to_all(outgoing, ("enc", "pool"), split_axis=1, concat_axis=1, tiled=True)
    slotted = arrived.reshape(tok, items_dev, width)
    values = slotted.astype(jnp.float32)
    normed = (values / jnp.sqrt(jnp.sum(values * values, axis=-1, keepdims=True) + 1e-06)).astype(
        jnp.bfloat16
    )
    position = jnp.arange(tok, dtype=jnp.int32)[None, :]
    valid = (position < lengths[:, None]) & ((position == 0) | (token_mask == 1))
    valid_tm = jnp.transpose(valid.reshape(items_dev, n_enc, toks), (2, 1, 0)).reshape(tok, items_dev)
    bias = jnp.where(valid_tm, 0.0, -4.0).astype(jnp.bfloat16)
    normed = lax.optimization_barrier(normed)
    normed = jnp.where(valid_tm[:, :, None], normed, normed[0][None])
    packed = jnp.concatenate([normed.reshape(n_tok, width), bias.reshape(-1, width)], axis=0)
    block = packed[:n_tok].reshape(tok, items_dev, width)

    parity = (pool_index ^ (pool_index >> 1) ^ (pool_index >> 2)) & 1
    is_a = (pool_index & 1) == 0

    def par(p):
        return (p ^ (p >> 1) ^ (p >> 2)) & 1

    send_pairs = [(p, p ^ (4 if par(p) else 2)) for p in range(n_pool)]
    back_pairs = [(t, s) for s, t in send_pairs]
    chip_pairs = [(p, p ^ 1) for p in range(n_pool)]

    z_recv = lax.ppermute(packed, "pool", send_pairs)
    c_recv = lax.ppermute(packed, "pool", chip_pairs)

    def row_flags(valid_rows):
        return jnp.broadcast_to(valid_rows.astype(jnp.float32).reshape(-1, 1), (valid_rows.size, 128))

    half = items_dev // 2
    own_flags = row_flags(valid_tm)
    c_blk = c_recv[:n_tok].reshape(tok, items_dev, width)
    c_valid = c_recv[n_tok:].reshape(tok, items_dev) == 0
    query = jnp.where(is_a, block[:, :half], c_blk[:, half:]).reshape(tok * half, width)
    query_flags = row_flags(jnp.where(is_a, valid_tm[:, :half], c_valid[:, half:]))
    other_packed = jnp.where(is_a, c_recv, packed)
    part, _ = chamfer_tile(query, query_flags, other_packed, tok)
    part, own_flags = lax.optimization_barrier((part, own_flags))
    part_recv = lax.ppermute(part, "pool", chip_pairs)
    joined = jnp.where(
        is_a,
        jnp.concatenate([part, part_recv], axis=0),
        jnp.concatenate([part_recv, part], axis=0),
    )
    tile0 = jnp.where(is_a, joined, joined.T)

    tile_z, tile_z_t = chamfer_tile(packed, own_flags, z_recv, tok)
    tile_back = lax.ppermute(tile_z_t, "pool", back_pairs)
    ready = lax.optimization_barrier(jnp.concatenate([tile0, tile_z, tile_z], axis=1))
    column = jnp.arange(3 * items_dev, dtype=jnp.int32)[None, :] // items_dev
    return jnp.where(column == 1 + parity, jnp.tile(tile_back, (1, 3)), ready)


def solution(mesh):
    in_specs = (P("pool", "enc", None), P(), P(("enc", "pool")), P(("enc", "pool"), None))
    out_specs = P(("enc", "pool"), None)
    return jax.shard_map(shards, mesh=mesh, in_specs=in_specs, out_specs=out_specs, check_vma=False)
```

```python
import functools

import jax
import jax.numpy as jnp
from jax import lax
from jax.experimental import pallas as pl
from jax.experimental.pallas import tpu as pltpu
from jax.sharding import PartitionSpec as P


def tile_scores(query, query_bias, other, other_bias):
    tok, query_items, width = query.shape
    other_items = other.shape[1]
    rows = min(32, query_items)
    blocks = query_items // rows
    other_flat = other.reshape(tok * other_items, width)
    other_add = other_bias.astype(jnp.float32)[:, :, None]
    other_valid = other_bias == 0
    turned_all = jnp.transpose(query.reshape(tok, blocks, rows, width), (1, 0, 2, 3))
    adding_all = jnp.transpose(query_bias.astype(jnp.float32).reshape(tok, blocks, rows), (1, 0, 2))[..., None]
    kept_all = jnp.transpose((query_bias == 0).reshape(tok, blocks, rows), (1, 0, 2))

    def one_block(operands):
        turned, adding, kept = operands
        flat = turned.reshape(tok * rows, width)
        dots_fore = jnp.einsum("ubh,qh->ubq", other, flat, preferred_element_type=jnp.float32)
        fore = jnp.max(dots_fore + other_add, axis=0).reshape(other_items, tok, rows)
        fore = jnp.sum(jnp.where(kept[None], fore, 0.0), axis=1)
        dots_back = jnp.einsum("trh,ch->trc", turned, other_flat, preferred_element_type=jnp.float32)
        back = jnp.max(dots_back + adding, axis=0).reshape(rows, tok, other_items)
        back = jnp.sum(jnp.where(other_valid[None], back, 0.0), axis=1)
        return 0.5 * (fore.T + back)

    result = lax.map(one_block, (turned_all, adding_all, kept_all))
    return result.reshape(query_items, other_items)


def _chamfer_kernel(tok, nq, no, cw, q_ref, o_ref, qv_ref, out_ref, out_t_ref, fm_ref):
    q = q_ref[0:tok * nq, :]
    n_rows = tok * no // 128
    flags = o_ref[tok * no:tok * no + n_rows, :].astype(jnp.float32)
    acc_b = jnp.zeros((nq, 128), jnp.float32)
    for c in range(tok * no // cw):
        o_c = o_ref[c * cw:(c + 1) * cw, :]
        d = lax.dot_general(q, o_c, (((1,), (1,)), ((), ())), preferred_element_type=jnp.float32)
        m = d[:, 0:128]
        for k in range(1, cw // 128):
            m = jnp.maximum(m, d[:, k * 128:(k + 1) * 128])
        if c == 0:
            fm_ref[...] = m
        else:
            fm_ref[...] = jnp.maximum(fm_ref[...], m)
        mb = jnp.max(d.reshape(tok, nq, cw), axis=0)
        for k in range(cw // 128):
            row = c * (cw // 128) + k
            acc_b = acc_b + jnp.where(flags[row:row + 1, :] == 0, mb[:, k * 128:(k + 1) * 128], 0.0)
    fm = fm_ref[...]
    fm = jnp.maximum(fm, pltpu.roll(fm, 64, 1))
    fsum = jnp.sum(jnp.where(qv_ref[...] > 0, fm, 0.0).reshape(tok, nq, 128), axis=0)
    bsum = acc_b + pltpu.roll(acc_b, 64, 1)
    res = 0.5 * (fsum + bsum)
    out_ref[...] = res[:, :no]
    out_t_ref[...] = res.T[:no, :]


def chamfer_tile(query, query_valid, other_packed, tok):
    tok_nq, width = query_valid.shape[0], query.shape[1]
    nq = tok_nq // tok
    no = 64
    cw = 512
    kernel = functools.partial(_chamfer_kernel, tok, nq, no, cw)
    return pl.pallas_call(
        kernel,
        out_shape=(jax.ShapeDtypeStruct((nq, no), jnp.float32), jax.ShapeDtypeStruct((no, nq), jnp.float32)),
        in_specs=[pl.BlockSpec(memory_space=pltpu.VMEM)] * 3,
        out_specs=(pl.BlockSpec(memory_space=pltpu.VMEM), pl.BlockSpec(memory_space=pltpu.VMEM)),
        scratch_shapes=[pltpu.VMEM((tok_nq, 128), jnp.float32)],
        compiler_params=pltpu.CompilerParams(vmem_limit_bytes=24 * 1024 * 1024),
        cost_estimate=pl.CostEstimate(
            flops=2 * tok_nq * tok * no * width, transcendentals=0, bytes_accessed=(tok_nq + tok * no) * width * 2
        ),
    )(query, other_packed, query_valid)


def shards(encoded, slot_items, lengths, token_mask):
    n_enc = lax.axis_size("enc")
    n_pool = lax.axis_size("pool")
    owners = n_enc * n_pool
    group = encoded.shape[0]
    toks = encoded.shape[1]
    width = encoded.shape[2]
    items_dev = lengths.shape[0]
    per = items_dev // n_pool
    tok = n_enc * toks
    n_tok = items_dev * tok
    pool_index = lax.axis_index("pool")

    table = slot_items.reshape(owners, n_pool, per)
    mine = lax.dynamic_index_in_dim(table, pool_index, 1, keepdims=False) - pool_index * group
    outgoing = jnp.take(encoded, mine, axis=0, mode="clip")
    arrived = lax.all_to_all(outgoing, ("enc", "pool"), split_axis=0, concat_axis=0, tiled=True)
    arrived = arrived.reshape(n_enc, n_pool, per, toks, width)
    slotted = jnp.transpose(arrived, (3, 0, 1, 2, 4)).reshape(tok, items_dev, width)
    values = slotted.astype(jnp.float32)
    normed = (values / jnp.sqrt(jnp.sum(values * values, axis=-1, keepdims=True) + 1e-06)).astype(
        jnp.bfloat16
    )
    position = jnp.arange(tok, dtype=jnp.int32)[None, :]
    valid = (position < lengths[:, None]) & ((position == 0) | (token_mask == 1))
    valid_tm = jnp.transpose(valid.reshape(items_dev, n_enc, toks), (2, 1, 0)).reshape(tok, items_dev)
    bias = jnp.where(valid_tm, 0.0, -4.0).astype(jnp.bfloat16)
    normed = lax.optimization_barrier(normed)
    normed = jnp.where(valid_tm[:, :, None], normed, normed[0][None])
    packed = jnp.concatenate([normed.reshape(n_tok, width), bias.reshape(-1, width)], axis=0)
    block = packed[:n_tok].reshape(tok, items_dev, width)

    parity = (pool_index ^ (pool_index >> 1) ^ (pool_index >> 2)) & 1
    is_a = (pool_index & 1) == 0

    def par(p):
        return (p ^ (p >> 1) ^ (p >> 2)) & 1

    send_pairs = [(p, p ^ (4 if par(p) else 2)) for p in range(n_pool)]
    back_pairs = [(t, s) for s, t in send_pairs]
    chip_pairs = [(p, p ^ 1) for p in range(n_pool)]

    z_recv = lax.ppermute(packed, "pool", send_pairs)
    c_recv = lax.ppermute(packed, "pool", chip_pairs)

    def row_flags(valid_rows):
        return jnp.broadcast_to(valid_rows.astype(jnp.float32).reshape(-1, 1), (valid_rows.size, 128))

    half = items_dev // 2
    own_flags = row_flags(valid_tm)
    c_blk = c_recv[:n_tok].reshape(tok, items_dev, width)
    c_valid = c_recv[n_tok:].reshape(tok, items_dev) == 0
    query = jnp.where(is_a, block[:, :half], c_blk[:, half:]).reshape(tok * half, width)
    query_flags = row_flags(jnp.where(is_a, valid_tm[:, :half], c_valid[:, half:]))
    other_packed = jnp.where(is_a, c_recv, packed)
    part, _ = chamfer_tile(query, query_flags, other_packed, tok)
    part, own_flags = lax.optimization_barrier((part, own_flags))
    part_recv = lax.ppermute(part, "pool", chip_pairs)
    joined = jnp.where(
        is_a,
        jnp.concatenate([part, part_recv], axis=0),
        jnp.concatenate([part_recv, part], axis=0),
    )
    tile0 = jnp.where(is_a, joined, joined.T)

    tile_z, tile_z_t = chamfer_tile(packed, own_flags, z_recv, tok)
    tile_back = lax.ppermute(tile_z_t, "pool", back_pairs)
    ready = lax.optimization_barrier(jnp.concatenate([tile0, tile_z, tile_z], axis=1))
    column = jnp.arange(3 * items_dev, dtype=jnp.int32)[None, :] // items_dev
    return jnp.where(column == 1 + parity, jnp.tile(tile_back, (1, 3)), ready)


def solution(mesh):
    in_specs = (P("pool", "enc", None), P(), P(("enc", "pool")), P(("enc", "pool"), None))
    out_specs = P(("enc", "pool"), None)
    return jax.shard_map(shards, mesh=mesh, in_specs=in_specs, out_specs=out_specs, check_vma=False)
```

```python
import functools

import jax
import jax.numpy as jnp
from jax import lax
from jax.experimental import pallas as pl
from jax.experimental.pallas import tpu as pltpu
from jax.sharding import PartitionSpec as P


def tile_scores(query, query_bias, other, other_bias):
    tok, query_items, width = query.shape
    other_items = other.shape[1]
    rows = min(32, query_items)
    blocks = query_items // rows
    other_flat = other.reshape(tok * other_items, width)
    other_add = other_bias.astype(jnp.float32)[:, :, None]
    other_valid = other_bias == 0
    turned_all = jnp.transpose(query.reshape(tok, blocks, rows, width), (1, 0, 2, 3))
    adding_all = jnp.transpose(query_bias.astype(jnp.float32).reshape(tok, blocks, rows), (1, 0, 2))[..., None]
    kept_all = jnp.transpose((query_bias == 0).reshape(tok, blocks, rows), (1, 0, 2))

    def one_block(operands):
        turned, adding, kept = operands
        flat = turned.reshape(tok * rows, width)
        dots_fore = jnp.einsum("ubh,qh->ubq", other, flat, preferred_element_type=jnp.float32)
        fore = jnp.max(dots_fore + other_add, axis=0).reshape(other_items, tok, rows)
        fore = jnp.sum(jnp.where(kept[None], fore, 0.0), axis=1)
        dots_back = jnp.einsum("trh,ch->trc", turned, other_flat, preferred_element_type=jnp.float32)
        back = jnp.max(dots_back + adding, axis=0).reshape(rows, tok, other_items)
        back = jnp.sum(jnp.where(other_valid[None], back, 0.0), axis=1)
        return 0.5 * (fore.T + back)

    result = lax.map(one_block, (turned_all, adding_all, kept_all))
    return result.reshape(query_items, other_items)


def _chamfer_kernel(tok, nq, no, cw, q_ref, o_ref, qv_ref, out_ref, out_t_ref, fm_ref):
    q = q_ref[0:tok * nq, :]
    n_rows = tok * no // 128
    flags = o_ref[tok * no:tok * no + n_rows, :].astype(jnp.float32)
    acc_b = jnp.zeros((nq, 128), jnp.float32)
    for c in range(tok * no // cw):
        o_c = o_ref[c * cw:(c + 1) * cw, :]
        d = lax.dot_general(q, o_c, (((1,), (1,)), ((), ())), preferred_element_type=jnp.float32)
        m = d[:, 0:128]
        for k in range(1, cw // 128):
            m = jnp.maximum(m, d[:, k * 128:(k + 1) * 128])
        if c == 0:
            fm_ref[...] = m
        else:
            fm_ref[...] = jnp.maximum(fm_ref[...], m)
        mb = jnp.max(d.reshape(tok, nq, cw), axis=0)
        for k in range(cw // 128):
            row = c * (cw // 128) + k
            acc_b = acc_b + jnp.where(flags[row:row + 1, :] == 0, mb[:, k * 128:(k + 1) * 128], 0.0)
    fm = fm_ref[...]
    fm = jnp.maximum(fm, pltpu.roll(fm, 64, 1))
    fsum = jnp.sum(jnp.where(qv_ref[...] > 0, fm, 0.0).reshape(tok, nq, 128), axis=0)
    bsum = acc_b + pltpu.roll(acc_b, 64, 1)
    res = 0.5 * (fsum + bsum)
    out_ref[...] = res[:, :no]
    out_t_ref[...] = res.T[:no, :]


def chamfer_tile(query, query_valid, other_packed, tok):
    tok_nq, width = query_valid.shape[0], query.shape[1]
    nq = tok_nq // tok
    no = 64
    cw = 512
    kernel = functools.partial(_chamfer_kernel, tok, nq, no, cw)
    return pl.pallas_call(
        kernel,
        out_shape=(jax.ShapeDtypeStruct((nq, no), jnp.float32), jax.ShapeDtypeStruct((no, nq), jnp.float32)),
        in_specs=[pl.BlockSpec(memory_space=pltpu.VMEM)] * 3,
        out_specs=(pl.BlockSpec(memory_space=pltpu.VMEM), pl.BlockSpec(memory_space=pltpu.VMEM)),
        scratch_shapes=[pltpu.VMEM((tok_nq, 128), jnp.float32)],
        compiler_params=pltpu.CompilerParams(vmem_limit_bytes=12 * 1024 * 1024),
        cost_estimate=pl.CostEstimate(
            flops=2 * tok_nq * tok * no * width, transcendentals=0, bytes_accessed=(tok_nq + tok * no) * width * 2
        ),
    )(query, other_packed, query_valid)


def shards(encoded, slot_items, lengths, token_mask):
    n_enc = lax.axis_size("enc")
    n_pool = lax.axis_size("pool")
    owners = n_enc * n_pool
    group = encoded.shape[0]
    toks = encoded.shape[1]
    width = encoded.shape[2]
    items_dev = lengths.shape[0]
    per = items_dev // n_pool
    tok = n_enc * toks
    n_tok = items_dev * tok
    pool_index = lax.axis_index("pool")

    table = slot_items.reshape(owners, n_pool, per)
    mine = lax.dynamic_index_in_dim(table, pool_index, 1, keepdims=False) - pool_index * group
    outgoing = jnp.take(encoded, mine, axis=0, mode="clip")
    outgoing = jnp.transpose(outgoing, (2, 0, 1, 3))
    arrived = lax.all_to_all(outgoing, ("enc", "pool"), split_axis=1, concat_axis=1, tiled=True)
    slotted = arrived.reshape(tok, items_dev, width)
    values = slotted.astype(jnp.float32)
    normed = (values / jnp.sqrt(jnp.sum(values * values, axis=-1, keepdims=True) + 1e-06)).astype(
        jnp.bfloat16
    )
    position = jnp.arange(tok, dtype=jnp.int32)[None, :]
    valid = (position < lengths[:, None]) & ((position == 0) | (token_mask == 1))
    valid_tm = jnp.transpose(valid.reshape(items_dev, n_enc, toks), (2, 1, 0)).reshape(tok, items_dev)
    bias = jnp.where(valid_tm, 0.0, -4.0).astype(jnp.bfloat16)
    normed = lax.optimization_barrier(normed)
    normed = jnp.where(valid_tm[:, :, None], normed, normed[0][None])
    packed = jnp.concatenate([normed.reshape(n_tok, width), bias.reshape(-1, width)], axis=0)
    block = packed[:n_tok].reshape(tok, items_dev, width)

    parity = (pool_index ^ (pool_index >> 1) ^ (pool_index >> 2)) & 1
    is_a = (pool_index & 1) == 0

    def par(p):
        return (p ^ (p >> 1) ^ (p >> 2)) & 1

    send_pairs = [(p, p ^ (4 if par(p) else 2)) for p in range(n_pool)]
    back_pairs = [(t, s) for s, t in send_pairs]
    chip_pairs = [(p, p ^ 1) for p in range(n_pool)]

    z_recv = lax.ppermute(packed, "pool", send_pairs)
    c_recv = lax.ppermute(packed, "pool", chip_pairs)

    def row_flags(valid_rows):
        return jnp.broadcast_to(valid_rows.astype(jnp.float32).reshape(-1, 1), (valid_rows.size, 128))

    half = items_dev // 2
    own_flags = row_flags(valid_tm)
    c_blk = c_recv[:n_tok].reshape(tok, items_dev, width)
    c_valid = c_recv[n_tok:].reshape(tok, items_dev) == 0
    query = jnp.where(is_a, block[:, :half], c_blk[:, half:]).reshape(tok * half, width)
    query_flags = row_flags(jnp.where(is_a, valid_tm[:, :half], c_valid[:, half:]))
    other_packed = jnp.where(is_a, c_recv, packed)
    part, _ = chamfer_tile(query, query_flags, other_packed, tok)
    part, own_flags = lax.optimization_barrier((part, own_flags))
    part_recv = lax.ppermute(part, "pool", chip_pairs)
    joined = jnp.where(
        is_a,
        jnp.concatenate([part, part_recv], axis=0),
        jnp.concatenate([part_recv, part], axis=0),
    )
    tile0 = jnp.where(is_a, joined, joined.T)

    tile_z, tile_z_t = chamfer_tile(packed, own_flags, z_recv, tok)
    tile_back = lax.ppermute(tile_z_t, "pool", back_pairs)
    ready = lax.optimization_barrier(jnp.concatenate([tile0, tile_z, tile_z], axis=1))
    column = jnp.arange(3 * items_dev, dtype=jnp.int32)[None, :] // items_dev
    return jnp.where(column == 1 + parity, jnp.tile(tile_back, (1, 3)), ready)


def solution(mesh):
    in_specs = (P("pool", "enc", None), P(), P(("enc", "pool")), P(("enc", "pool"), None))
    out_specs = P(("enc", "pool"), None)
    return jax.shard_map(shards, mesh=mesh, in_specs=in_specs, out_specs=out_specs, check_vma=False)
```

```python
import functools

import jax
import jax.numpy as jnp
from jax import lax
from jax.experimental import pallas as pl
from jax.experimental.pallas import tpu as pltpu
from jax.sharding import PartitionSpec as P


def tile_scores(query, query_bias, other, other_bias):
    tok, query_items, width = query.shape
    other_items = other.shape[1]
    rows = min(32, query_items)
    blocks = query_items // rows
    other_flat = other.reshape(tok * other_items, width)
    other_add = other_bias.astype(jnp.float32)[:, :, None]
    other_valid = other_bias == 0
    turned_all = jnp.transpose(query.reshape(tok, blocks, rows, width), (1, 0, 2, 3))
    adding_all = jnp.transpose(query_bias.astype(jnp.float32).reshape(tok, blocks, rows), (1, 0, 2))[..., None]
    kept_all = jnp.transpose((query_bias == 0).reshape(tok, blocks, rows), (1, 0, 2))

    def one_block(operands):
        turned, adding, kept = operands
        flat = turned.reshape(tok * rows, width)
        dots_fore = jnp.einsum("ubh,qh->ubq", other, flat, preferred_element_type=jnp.float32)
        fore = jnp.max(dots_fore + other_add, axis=0).reshape(other_items, tok, rows)
        fore = jnp.sum(jnp.where(kept[None], fore, 0.0), axis=1)
        dots_back = jnp.einsum("trh,ch->trc", turned, other_flat, preferred_element_type=jnp.float32)
        back = jnp.max(dots_back + adding, axis=0).reshape(rows, tok, other_items)
        back = jnp.sum(jnp.where(other_valid[None], back, 0.0), axis=1)
        return 0.5 * (fore.T + back)

    result = lax.map(one_block, (turned_all, adding_all, kept_all))
    return result.reshape(query_items, other_items)


def _chamfer_kernel(tok, nq, no, cw, q_ref, o_ref, qv_ref, out_ref, out_t_ref, fm_ref):
    q = q_ref[0:tok * nq, :]
    n_rows = tok * no // 128
    flags = o_ref[tok * no:tok * no + n_rows, :].astype(jnp.float32)
    acc_b = jnp.zeros((nq, 128), jnp.float32)
    for c in range(tok * no // cw):
        o_c = o_ref[c * cw:(c + 1) * cw, :]
        d = lax.dot_general(q, o_c, (((1,), (1,)), ((), ())), preferred_element_type=jnp.float32)
        m = d[:, 0:128]
        for k in range(1, cw // 128):
            m = jnp.maximum(m, d[:, k * 128:(k + 1) * 128])
        if c == 0:
            fm_ref[...] = m
        else:
            fm_ref[...] = jnp.maximum(fm_ref[...], m)
        mb = jnp.max(d.reshape(tok, nq, cw), axis=0)
        for k in range(cw // 128):
            row = c * (cw // 128) + k
            acc_b = acc_b + jnp.where(flags[row:row + 1, :] == 0, mb[:, k * 128:(k + 1) * 128], 0.0)
    fm = fm_ref[...]
    fm = jnp.maximum(fm, pltpu.roll(fm, 64, 1))
    fsum = jnp.sum(jnp.where(qv_ref[...] > 0, fm, 0.0).reshape(tok, nq, 128), axis=0)
    bsum = acc_b + pltpu.roll(acc_b, 64, 1)
    res = 0.5 * (fsum + bsum)
    out_ref[...] = res[:, :no]
    out_t_ref[...] = res.T[:no, :]


def chamfer_tile(query, query_valid, other_packed, tok):
    tok_nq, width = query_valid.shape[0], query.shape[1]
    nq = tok_nq // tok
    no = 64
    cw = 512
    kernel = functools.partial(_chamfer_kernel, tok, nq, no, cw)
    return pl.pallas_call(
        kernel,
        out_shape=(jax.ShapeDtypeStruct((nq, no), jnp.float32), jax.ShapeDtypeStruct((no, nq), jnp.float32)),
        in_specs=[pl.BlockSpec(memory_space=pltpu.VMEM)] * 3,
        out_specs=(pl.BlockSpec(memory_space=pltpu.VMEM), pl.BlockSpec(memory_space=pltpu.VMEM)),
        scratch_shapes=[pltpu.VMEM((tok_nq, 128), jnp.float32)],
        compiler_params=pltpu.CompilerParams(vmem_limit_bytes=24 * 1024 * 1024),
        cost_estimate=pl.CostEstimate(
            flops=2 * tok_nq * tok * no * width, transcendentals=0, bytes_accessed=(tok_nq + tok * no) * width * 2
        ),
    )(query, other_packed, query_valid)


def shards(encoded, slot_items, lengths, token_mask):
    n_enc = lax.axis_size("enc")
    n_pool = lax.axis_size("pool")
    owners = n_enc * n_pool
    group = encoded.shape[0]
    toks = encoded.shape[1]
    width = encoded.shape[2]
    items_dev = lengths.shape[0]
    per = items_dev // n_pool
    tok = n_enc * toks
    n_tok = items_dev * tok
    pool_index = lax.axis_index("pool")

    table = slot_items.reshape(owners, n_pool, per)
    mine = lax.dynamic_index_in_dim(table, pool_index, 1, keepdims=False) - pool_index * group
    outgoing = jnp.take(encoded, mine, axis=0, mode="clip")
    outgoing = jnp.transpose(outgoing, (2, 0, 1, 3))
    arrived = lax.all_to_all(outgoing, ("enc", "pool"), split_axis=1, concat_axis=1, tiled=True)
    slotted = arrived.reshape(tok, items_dev, width)
    values = slotted.astype(jnp.float32)
    normed = (values / jnp.sqrt(jnp.sum(values * values, axis=-1, keepdims=True) + 1e-06)).astype(
        jnp.bfloat16
    )
    position = jnp.arange(tok, dtype=jnp.int32)[None, :]
    valid = (position < lengths[:, None]) & ((position == 0) | (token_mask == 1))
    valid_tm = jnp.transpose(valid.reshape(items_dev, n_enc, toks), (2, 1, 0)).reshape(tok, items_dev)
    bias = jnp.where(valid_tm, 0.0, -4.0).astype(jnp.bfloat16)
    normed = lax.optimization_barrier(normed)
    normed = jnp.where(valid_tm[:, :, None], normed, normed[0][None])
    packed = jnp.concatenate([normed.reshape(n_tok, width), bias.reshape(-1, width)], axis=0)
    block = packed[:n_tok].reshape(tok, items_dev, width)

    parity = (pool_index ^ (pool_index >> 1) ^ (pool_index >> 2)) & 1
    is_a = (pool_index & 1) == 0

    def par(p):
        return (p ^ (p >> 1) ^ (p >> 2)) & 1

    send_pairs = [(p, p ^ (4 if par(p) else 2)) for p in range(n_pool)]
    back_pairs = [(t, s) for s, t in send_pairs]
    chip_pairs = [(p, p ^ 1) for p in range(n_pool)]

    z_recv = lax.ppermute(packed, "pool", send_pairs)
    c_recv = lax.ppermute(packed, "pool", chip_pairs)

    def row_flags(valid_rows):
        return jnp.broadcast_to(valid_rows.astype(jnp.float32).reshape(-1, 1), (valid_rows.size, 128))

    half = items_dev // 2
    own_flags = row_flags(valid_tm)
    c_blk = c_recv[:n_tok].reshape(tok, items_dev, width)
    c_valid = c_recv[n_tok:].reshape(tok, items_dev) == 0
    query = jnp.where(is_a, block[:, :half], c_blk[:, half:]).reshape(tok * half, width)
    query_flags = row_flags(jnp.where(is_a, valid_tm[:, :half], c_valid[:, half:]))
    other_packed = jnp.where(is_a, c_recv, packed)
    part, _ = chamfer_tile(query, query_flags, other_packed, tok)
    part, own_flags = lax.optimization_barrier((part, own_flags))
    part_recv = lax.ppermute(part, "pool", chip_pairs)
    joined = jnp.where(
        is_a,
        jnp.concatenate([part, part_recv], axis=0),
        jnp.concatenate([part_recv, part], axis=0),
    )
    tile0 = jnp.where(is_a, joined, joined.T)

    tile_z, tile_z_t = chamfer_tile(packed, own_flags, z_recv, tok)
    tile_back = lax.ppermute(jnp.tile(tile_z_t, (1, 3)), "pool", back_pairs)
    ready = lax.optimization_barrier(jnp.concatenate([tile0, tile_z, tile_z], axis=1))
    column = jnp.arange(3 * items_dev, dtype=jnp.int32)[None, :] // items_dev
    return jnp.where(column == 1 + parity, tile_back, ready)


def solution(mesh):
    in_specs = (P("pool", "enc", None), P(), P(("enc", "pool")), P(("enc", "pool"), None))
    out_specs = P(("enc", "pool"), None)
    return jax.shard_map(shards, mesh=mesh, in_specs=in_specs, out_specs=out_specs, check_vma=False)
```
